256 devices in a mesh: probe: 16 (over z, x_lo), slab: 16 (over x_hi, y, core).
Axes of the slice: x: 4 (x_hi: 2, x_lo: 2; x = x_hi * 2 + x_lo), y: 4, z: 8, core: 2. Of those that a mesh axis runs over, the one named last changes fastest.
Arguments:
- u_prev: float32 [512, 128, 128], P('slab', 'probe'), may hold values from -6 to 6
- u_cur: float32 [512, 128, 128], P('slab', 'probe'), may hold values from -6 to 6
- buoyancy: float32 [512, 128, 128], P('slab'), may hold values from 0.6 to 1.4
- kappa: float32 [512, 128, 128], P('slab'), may hold values from 0.06 to 0.14
- dkappa: float32 [16, 512, 128, 128], P('probe', 'slab'), may hold values from -0.3 to 0.3
- du_prev: float32 [16, 512, 128, 128], P('probe', 'slab'), may hold values from -6 to 6
- du_cur: float32 [16, 512, 128, 128], P('probe', 'slab'), may hold values from -6 to 6
Outputs:
- background_first: float32 [512, 128, 128], P('slab', 'probe')
- background_second: float32 [512, 128, 128], P('slab', 'probe')
- born_first: float32 [16, 512, 128, 128], P('probe', 'slab')
- born_second: float32 [16, 512, 128, 128], P('probe', 'slab')
The draws below stay inside these ranges and needn't reach their ends.
All inputs are finite; a program needn't handle non-finite values.
Results may differ from the reference program's by a relative error of at most 0.00002.
Values sent between devices are 32-bit elements; how exact they have to be, the bound alone decides.
No kernel may reach another device: no remote copies, remote signals or barrier semaphores. Data moves between devices by JAX's collectives and lax.ppermute only.
A program may use at most 128 MiB of HBM per device.

```python
import math
import jax
import jax.numpy as jnp
from jax import lax

NY = 128
NZ = 512
NX = 128
PROBES = 16


def steps_of(own_key, dims, pieces, least, top_value):
    def one(axis_at, shards_of):
        draws = jax.random.uniform(jax.random.fold_in(jax.random.fold_in(own_key, 6), axis_at), (shards_of,), jnp.float32, least / len(pieces), top_value / len(pieces))
        return jnp.repeat(jnp.exp(draws), dims[axis_at] // shards_of).reshape((-1,) + (1,) * (len(dims) - axis_at - 1))

    factor_of = one(*pieces[0])
    for cut in pieces[1:]:
        factor_of = factor_of * one(*cut)
    return factor_of


def scatter_about(stream_key, shape, spread, bound, split=(), held_as=jnp.bfloat16):
    values = spread * jax.random.normal(stream_key, shape, jnp.float32)
    if split:
        values = values * steps_of(stream_key, shape, split, -0.22, 0.18)
    return jnp.clip(values, -bound, bound).astype(held_as)


def setup_inputs(seed: int = 0) -> dict:
    keys = jax.random.split(jax.random.key(seed), 8)
    u_prev = scatter_about(keys[0], (NZ, NX, NY), 1.0, 6.0, ((0, 16), (1, 16)), jnp.float32)
    u_cur = scatter_about(keys[1], (NZ, NX, NY), 1.0, 6.0, ((0, 16), (1, 16)), jnp.float32)
    buoyancy = jnp.clip(0.6 + 0.79999995 * jax.random.uniform(keys[2], (NZ, NX, NY), jnp.float32) ** steps_of(keys[2], (NZ, NX, NY), ((0, 16),), -0.2, 0.2), 0.6, 1.4)
    kappa = jnp.clip(jnp.exp(math.log(0.14) - 0.8472979 * jax.random.uniform(keys[3], (NZ, NX, NY), jnp.float32) ** steps_of(keys[3], (NZ, NX, NY), ((0, 16),), -0.2, 0.2)), 0.06, 0.14)
    dkappa = scatter_about(keys[4], (PROBES, NZ, NX, NY), 0.05, 0.3, ((0, 16), (1, 16)), jnp.float32)
    du_prev = scatter_about(keys[5], (PROBES, NZ, NX, NY), 1.0, 6.0, ((0, 16), (1, 16)), jnp.float32)
    du_cur = scatter_about(keys[6], (PROBES, NZ, NX, NY), 1.0, 6.0, ((0, 16), (1, 16)), jnp.float32)
    return {"u_prev": u_prev, "u_cur": u_cur, "buoyancy": buoyancy, "kappa": kappa, "dkappa": dkappa, "du_prev": du_prev, "du_cur": du_cur}


SECOND = (-205.0 / 72.0, 8.0 / 5.0, -1.0 / 5.0, 8.0 / 315.0, -1.0 / 560.0)
FIRST = (0.0, 4.0 / 5.0, -1.0 / 5.0, 4.0 / 105.0, -1.0 / 280.0)


def derivatives(extended):
    array_rank = extended.ndim
    center = extended[..., 4:-4, 4:-4, 4:-4]
    cores = (extended[..., :, 4:-4, 4:-4], extended[..., 4:-4, :, 4:-4], extended[..., 4:-4, 4:-4, :])
    second = 3.0 * SECOND[0] * center
    gradients = []
    for dimension in range(3):
        source = cores[dimension]
        axis_place = array_rank - 3 + dimension
        extent = center.shape[axis_place]
        gradient = jnp.zeros_like(center)
        for distance in range(1, 5):
            higher = lax.slice_in_dim(source, 4 + distance, 4 + distance + extent, axis=axis_place)
            deeper = lax.slice_in_dim(source, 4 - distance, 4 - distance + extent, axis=axis_place)
            second = second + SECOND[distance] * (higher + deeper)
            gradient = gradient + FIRST[distance] * (higher - deeper)
        gradients.append(gradient)
    return second, gradients[0], gradients[1], gradients[2]


def operate(extended, buoyancy, slopes):
    second, depth_slope, cross_slope, lateral_slope = derivatives(extended)
    return buoyancy * second + slopes[0] * depth_slope + slopes[1] * cross_slope + slopes[2] * lateral_slope


def reference(u_prev, u_cur, buoyancy, kappa, dkappa, du_prev, du_cur):
    unused, slope_one, slope_two, slope_three = derivatives(jnp.pad(buoyancy, 4))
    slopes = (slope_one, slope_two, slope_three)

    def apply_operator(field):
        return operate(jnp.pad(field, 4), buoyancy, slopes)

    image_first = apply_operator(u_cur)
    background_first = 2.0 * u_cur - u_prev + kappa * image_first
    image_second = apply_operator(background_first)
    background_second = 2.0 * background_first - u_cur + kappa * image_second

    def born(items):
        probe_kappa, older, newer = items
        one_step = 2.0 * newer - older + kappa * apply_operator(newer) + probe_kappa * image_first
        two_steps = 2.0 * one_step - newer + kappa * apply_operator(one_step) + probe_kappa * image_second
        return one_step, two_steps

    born_first, born_second = lax.map(born, (dkappa, du_prev, du_cur))
    return background_first, background_second, born_first, born_second
```

```python
import functools

import numpy as np
import jax
import jax.numpy as jnp
from jax import lax
from jax.experimental import pallas as pl
from jax.experimental.pallas import tpu as pltpu
from jax.sharding import PartitionSpec as P

SECOND = (-205.0 / 72.0, 8.0 / 5.0, -1.0 / 5.0, 8.0 / 315.0, -1.0 / 560.0)
FIRST = (0.0, 4.0 / 5.0, -1.0 / 5.0, 4.0 / 105.0, -1.0 / 280.0)

BZ = 8
HALO = 4
INTERPRET = False
HI = lax.Precision.HIGHEST


def band_matrices(n):
    ms = np.zeros((n, n), np.float32)
    mg = np.zeros((n, n), np.float32)
    for i in range(n):
        for k in range(1, 5):
            for j, sign in ((i + k, 1.0), (i - k, -1.0)):
                if 0 <= j < n:
                    ms[i, j] = SECOND[k]
                    mg[i, j] = sign * FIRST[k]
    return ms, mg


def halo_depth(cells):
    count = lax.axis_size("slab")
    ends = count - 1
    head = cells[:HALO]
    tail = cells[cells.shape[0] - HALO:]
    return jnp.concatenate(
        [
            lax.ppermute(tail, "slab", [(i, i + 1) for i in range(ends)]),
            cells,
            lax.ppermute(head, "slab", [(i + 1, i) for i in range(ends)]),
        ],
        axis=0,
    )


def _ext(lo_ref, hi_ref, idx):
    if idx < BZ:
        return lo_ref[idx]
    return hi_ref[idx - BZ]


def _depth_terms(lo_ref, hi_ref, j):
    c = j + HALO
    centre = _ext(lo_ref, hi_ref, c)
    second = (3.0 * SECOND[0]) * centre
    grad = None
    for k in range(1, 5):
        up = _ext(lo_ref, hi_ref, c + k)
        down = _ext(lo_ref, hi_ref, c - k)
        second = second + SECOND[k] * (up + down)
        term = FIRST[k] * (up - down)
        grad = term if grad is None else grad + term
    return centre, second, grad


def _slope_kernel(lo_ref, hi_ref, mlane_ref, msub_ref, g0_ref, g1_ref, g2_ref):
    n = mlane_ref.shape[0]
    for j in range(BZ):
        centre, _, grad = _depth_terms(lo_ref, hi_ref, j)
        lane = jnp.dot(centre, mlane_ref[...], precision=HI, preferred_element_type=jnp.float32)
        sub = jnp.dot(msub_ref[...], centre, precision=HI, preferred_element_type=jnp.float32)
        g0_ref[j] = grad
        g1_ref[j] = sub[n:]
        g2_ref[j] = lane[:, n:]


def _op_kernel(flags, *refs):
    with_prev, with_img, want_image, want_step = flags
    refs = list(refs)
    lo_ref, hi_ref, b_ref, g0_ref, g1_ref, g2_ref, mlane_ref, msub_ref = refs[:8]
    rest = refs[8:]
    kappa_ref = prev_ref = dk_ref = img_ref = None
    if want_step:
        kappa_ref = rest.pop(0)
        if with_prev:
            prev_ref = rest.pop(0)
        if with_img:
            dk_ref = rest.pop(0)
            img_ref = rest.pop(0)
    outs = rest
    n = mlane_ref.shape[0]
    for j in range(BZ):
        centre, second, grad = _depth_terms(lo_ref, hi_ref, j)
        lane = jnp.dot(centre, mlane_ref[...], precision=HI, preferred_element_type=jnp.float32)
        sub = jnp.dot(msub_ref[...], centre, precision=HI, preferred_element_type=jnp.float32)
        second = second + sub[:n] + lane[:, :n]
        image = (
            b_ref[j] * second
            + g0_ref[j] * grad
            + g1_ref[j] * sub[n:]
            + g2_ref[j] * lane[:, n:]
        )
        at = 0
        if want_image:
            outs[at][j] = image
            at += 1
        if want_step:
            step = 2.0 * centre + kappa_ref[j] * image
            if with_prev:
                step = step - prev_ref[j]
            if with_img:
                step = step + dk_ref[j] * img_ref[j]
            outs[at][j] = step


def _specs(n, count):
    blk = pl.BlockSpec((BZ, n, n), lambda i: (i, 0, 0))
    return [blk] * count


def _ext_specs(n):
    return [
        pl.BlockSpec((BZ, n, n), lambda i: (i, 0, 0)),
        pl.BlockSpec((BZ, n, n), lambda i: (i + 1, 0, 0)),
    ]


def _mat_specs(n):
    return [
        pl.BlockSpec((n, 2 * n), lambda i: (0, 0)),
        pl.BlockSpec((2 * n, n), lambda i: (0, 0)),
    ]


def slopes_of(b_ext, mlane, msub):
    depth = b_ext.shape[0] - 2 * HALO
    n = b_ext.shape[1]
    shape = jax.ShapeDtypeStruct((depth, n, n), jnp.float32)
    return pl.pallas_call(
        _slope_kernel,
        grid=(depth // BZ,),
        in_specs=_ext_specs(n) + _mat_specs(n),
        out_specs=_specs(n, 3),
        out_shape=[shape] * 3,
        compiler_params=pltpu.CompilerParams(vmem_limit_bytes=48 * 1024 * 1024),
        interpret=INTERPRET,
    )(b_ext, b_ext, mlane, msub)


def apply_op(f_ext, b, slopes, mlane, msub, kappa=None, prev=None, dk=None, img=None, want_image=False):
    depth = f_ext.shape[0] - 2 * HALO
    n = f_ext.shape[1]
    want_step = kappa is not None
    with_prev = prev is not None
    with_img = img is not None
    args = [f_ext, f_ext, b, *slopes, mlane, msub]
    in_specs = _ext_specs(n) + _specs(n, 4) + _mat_specs(n)
    if want_step:
        extra = [kappa] + ([prev] if with_prev else []) + ([dk, img] if with_img else [])
        args += extra
        in_specs += _specs(n, len(extra))
    n_out = int(want_image) + int(want_step)
    shape = jax.ShapeDtypeStruct((depth, n, n), jnp.float32)
    outs = pl.pallas_call(
        functools.partial(_op_kernel, (with_prev, with_img, want_image, want_step)),
        grid=(depth // BZ,),
        in_specs=in_specs,
        out_specs=_specs(n, n_out),
        out_shape=[shape] * n_out,
        compiler_params=pltpu.CompilerParams(vmem_limit_bytes=48 * 1024 * 1024),
        interpret=INTERPRET,
    )(*args)
    return outs


def local(u_prev, u_cur, buoyancy, kappa, dkappa, du_prev, du_cur):
    n = buoyancy.shape[1]
    strip = u_cur.shape[1]
    offset = lax.axis_index("probe") * strip
    ms, mg = band_matrices(n)
    mlane = jnp.asarray(np.concatenate([ms, mg.T], axis=1))
    msub = jnp.asarray(np.concatenate([ms, mg], axis=0))

    u_cur_ext = lax.all_gather(halo_depth(u_cur), "probe", axis=1, tiled=True)
    u_prev_all = lax.all_gather(u_prev, "probe", axis=1, tiled=True)

    slopes = slopes_of(halo_depth(buoyancy), mlane, msub)

    probe_kappa = dkappa[0]
    older = du_prev[0]
    newer = du_cur[0]

    (partial_first,) = apply_op(halo_depth(newer), buoyancy, slopes, mlane, msub, kappa=kappa, prev=older)

    image_first, background_first = apply_op(
        u_cur_ext, buoyancy, slopes, mlane, msub, kappa=kappa, prev=u_prev_all, want_image=True
    )
    born_first = partial_first + probe_kappa * image_first

    (image_second,) = apply_op(halo_depth(background_first), buoyancy, slopes, mlane, msub, want_image=True)

    def cut_strip(field):
        return lax.dynamic_slice_in_dim(field, offset, strip, 1)

    background_first_strip = cut_strip(background_first)
    background_second = (
        2.0 * background_first_strip - u_cur + cut_strip(kappa) * cut_strip(image_second)
    )

    (born_second,) = apply_op(
        halo_depth(born_first), buoyancy, slopes, mlane, msub,
        kappa=kappa, prev=newer, dk=probe_kappa, img=image_second,
    )
    return background_first_strip, background_second, born_first[None], born_second[None]


def solution(mesh):
    return jax.shard_map(
        local,
        mesh=mesh,
        in_specs=(
            P("slab", "probe", None),
            P("slab", "probe", None),
            P("slab", None, None),
            P("slab", None, None),
            P("probe", "slab", None, None),
            P("probe", "slab", None, None),
            P("probe", "slab", None, None),
        ),
        out_specs=(
            P("slab", "probe", None),
            P("slab", "probe", None),
            P("probe", "slab", None, None),
            P("probe", "slab", None, None),
        ),
        check_vma=False,
    )
```

```python
import functools

import numpy as np
import jax
import jax.numpy as jnp
from jax import lax
from jax.experimental import pallas as pl
from jax.experimental.pallas import tpu as pltpu
from jax.sharding import PartitionSpec as P

SECOND = (-205.0 / 72.0, 8.0 / 5.0, -1.0 / 5.0, 8.0 / 315.0, -1.0 / 560.0)
FIRST = (0.0, 4.0 / 5.0, -1.0 / 5.0, 4.0 / 105.0, -1.0 / 280.0)

BZ = 8
HALO = 4
INTERPRET = False
HI = lax.Precision.HIGHEST


def band_matrices(n):
    ms = np.zeros((n, n), np.float32)
    mg = np.zeros((n, n), np.float32)
    for i in range(n):
        for k in range(1, 5):
            for j, sign in ((i + k, 1.0), (i - k, -1.0)):
                if 0 <= j < n:
                    ms[i, j] = SECOND[k]
                    mg[i, j] = sign * FIRST[k]
    return ms, mg


def halo_depth(cells):
    count = lax.axis_size("slab")
    ends = count - 1
    head = cells[:HALO]
    tail = cells[cells.shape[0] - HALO:]
    return jnp.concatenate(
        [
            lax.ppermute(tail, "slab", [(i, i + 1) for i in range(ends)]),
            cells,
            lax.ppermute(head, "slab", [(i + 1, i) for i in range(ends)]),
        ],
        axis=0,
    )


def ring_gather(x):
    n = lax.axis_size("probe")
    rings = n // 2
    p = lax.axis_index("probe")
    partner = lax.ppermute(x, "probe", [(i, i ^ 1) for i in range(n)])
    pair = jnp.where(p % 2 == 0, jnp.concatenate([x, partner], 1), jnp.concatenate([partner, x], 1))
    ahead = [(i, (i + 2) % n) for i in range(n)]
    behind = [(i, (i - 2) % n) for i in range(n)]
    by_offset = {0: pair}
    fwd = pair
    bwd = pair
    half = rings // 2
    for k in range(1, half):
        fwd = lax.ppermute(fwd, "probe", ahead)
        bwd = lax.ppermute(bwd, "probe", behind)
        by_offset[-k % rings] = fwd
        by_offset[k] = bwd
    cut = x.shape[0] // 2
    far = jnp.concatenate(
        [lax.ppermute(fwd[:cut], "probe", ahead), lax.ppermute(bwd[cut:], "probe", behind)], axis=0
    )
    by_offset[half] = far
    ordered = jnp.concatenate([by_offset[d] for d in range(rings)] * 2, axis=1)
    width = pair.shape[1]
    start = ((rings - p // 2) % rings) * width
    return lax.dynamic_slice_in_dim(ordered, start, rings * width, 1)


def _ext(lo_ref, hi_ref, idx):
    if idx < BZ:
        return lo_ref[idx]
    return hi_ref[idx - BZ]


def _depth_terms(lo_ref, hi_ref, j):
    c = j + HALO
    centre = _ext(lo_ref, hi_ref, c)
    second = (3.0 * SECOND[0]) * centre
    grad = None
    for k in range(1, 5):
        up = _ext(lo_ref, hi_ref, c + k)
        down = _ext(lo_ref, hi_ref, c - k)
        second = second + SECOND[k] * (up + down)
        term = FIRST[k] * (up - down)
        grad = term if grad is None else grad + term
    return centre, second, grad


def _slope_kernel(lo_ref, hi_ref, mlane_ref, msub_ref, g0_ref, g1_ref, g2_ref):
    n = mlane_ref.shape[0]
    for j in range(BZ):
        centre, _, grad = _depth_terms(lo_ref, hi_ref, j)
        lane = jnp.dot(centre, mlane_ref[...], precision=HI, preferred_element_type=jnp.float32)
        sub = jnp.dot(msub_ref[...], centre, precision=HI, preferred_element_type=jnp.float32)
        g0_ref[j] = grad
        g1_ref[j] = sub[n:]
        g2_ref[j] = lane[:, n:]


def _op_kernel(flags, *refs):
    with_prev, with_img, want_image, want_step = flags
    refs = list(refs)
    lo_ref, hi_ref, b_ref, g0_ref, g1_ref, g2_ref, mlane_ref, msub_ref = refs[:8]
    rest = refs[8:]
    kappa_ref = prev_ref = dk_ref = img_ref = None
    if want_step:
        kappa_ref = rest.pop(0)
        if with_prev:
            prev_ref = rest.pop(0)
        if with_img:
            dk_ref = rest.pop(0)
            img_ref = rest.pop(0)
    outs = rest
    n = mlane_ref.shape[0]
    for j in range(BZ):
        centre, second, grad = _depth_terms(lo_ref, hi_ref, j)
        lane = jnp.dot(centre, mlane_ref[...], precision=HI, preferred_element_type=jnp.float32)
        sub = jnp.dot(msub_ref[...], centre, precision=HI, preferred_element_type=jnp.float32)
        second = second + sub[:n] + lane[:, :n]
        image = (
            b_ref[j] * second
            + g0_ref[j] * grad
            + g1_ref[j] * sub[n:]
            + g2_ref[j] * lane[:, n:]
        )
        at = 0
        if want_image:
            outs[at][j] = image
            at += 1
        if want_step:
            step = 2.0 * centre + kappa_ref[j] * image
            if with_prev:
                step = step - prev_ref[j]
            if with_img:
                step = step + dk_ref[j] * img_ref[j]
            outs[at][j] = step


def _specs(n, count):
    blk = pl.BlockSpec((BZ, n, n), lambda i: (i, 0, 0))
    return [blk] * count


def _ext_specs(n):
    return [
        pl.BlockSpec((BZ, n, n), lambda i: (i, 0, 0)),
        pl.BlockSpec((BZ, n, n), lambda i: (i + 1, 0, 0)),
    ]


def _mat_specs(n):
    return [
        pl.BlockSpec((n, 2 * n), lambda i: (0, 0)),
        pl.BlockSpec((2 * n, n), lambda i: (0, 0)),
    ]


def slopes_of(b_ext, mlane, msub):
    depth = b_ext.shape[0] - 2 * HALO
    n = b_ext.shape[1]
    shape = jax.ShapeDtypeStruct((depth, n, n), jnp.float32)
    return pl.pallas_call(
        _slope_kernel,
        grid=(depth // BZ,),
        in_specs=_ext_specs(n) + _mat_specs(n),
        out_specs=_specs(n, 3),
        out_shape=[shape] * 3,
        compiler_params=pltpu.CompilerParams(vmem_limit_bytes=48 * 1024 * 1024),
        interpret=INTERPRET,
    )(b_ext, b_ext, mlane, msub)


def apply_op(f_ext, b, slopes, mlane, msub, kappa=None, prev=None, dk=None, img=None, want_image=False):
    depth = f_ext.shape[0] - 2 * HALO
    n = f_ext.shape[1]
    want_step = kappa is not None
    with_prev = prev is not None
    with_img = img is not None
    args = [f_ext, f_ext, b, *slopes, mlane, msub]
    in_specs = _ext_specs(n) + _specs(n, 4) + _mat_specs(n)
    if want_step:
        extra = [kappa] + ([prev] if with_prev else []) + ([dk, img] if with_img else [])
        args += extra
        in_specs += _specs(n, len(extra))
    n_out = int(want_image) + int(want_step)
    shape = jax.ShapeDtypeStruct((depth, n, n), jnp.float32)
    outs = pl.pallas_call(
        functools.partial(_op_kernel, (with_prev, with_img, want_image, want_step)),
        grid=(depth // BZ,),
        in_specs=in_specs,
        out_specs=_specs(n, n_out),
        out_shape=[shape] * n_out,
        compiler_params=pltpu.CompilerParams(vmem_limit_bytes=48 * 1024 * 1024),
        interpret=INTERPRET,
    )(*args)
    return outs


def local(u_prev, u_cur, buoyancy, kappa, dkappa, du_prev, du_cur):
    n = buoyancy.shape[1]
    strip = u_cur.shape[1]
    offset = lax.axis_index("probe") * strip
    ms, mg = band_matrices(n)
    mlane = jnp.asarray(np.concatenate([ms, mg.T], axis=1))
    msub = jnp.asarray(np.concatenate([ms, mg], axis=0))

    depth = u_cur.shape[0]
    both = ring_gather(jnp.concatenate([halo_depth(u_cur), u_prev], axis=0))
    u_cur_ext = both[: depth + 2 * HALO]
    u_prev_all = both[depth + 2 * HALO:]

    slopes = slopes_of(halo_depth(buoyancy), mlane, msub)

    probe_kappa = dkappa[0]
    older = du_prev[0]
    newer = du_cur[0]

    (partial_first,) = apply_op(halo_depth(newer), buoyancy, slopes, mlane, msub, kappa=kappa, prev=older)

    image_first, background_first = apply_op(
        u_cur_ext, buoyancy, slopes, mlane, msub, kappa=kappa, prev=u_prev_all, want_image=True
    )
    born_first = partial_first + probe_kappa * image_first

    (image_second,) = apply_op(halo_depth(background_first), buoyancy, slopes, mlane, msub, want_image=True)

    def cut_strip(field):
        return lax.dynamic_slice_in_dim(field, offset, strip, 1)

    background_first_strip = cut_strip(background_first)
    background_second = (
        2.0 * background_first_strip - u_cur + cut_strip(kappa) * cut_strip(image_second)
    )

    (born_second,) = apply_op(
        halo_depth(born_first), buoyancy, slopes, mlane, msub,
        kappa=kappa, prev=newer, dk=probe_kappa, img=image_second,
    )
    return background_first_strip, background_second, born_first[None], born_second[None]


def solution(mesh):
    return jax.shard_map(
        local,
        mesh=mesh,
        in_specs=(
            P("slab", "probe", None),
            P("slab", "probe", None),
            P("slab", None, None),
            P("slab", None, None),
            P("probe", "slab", None, None),
            P("probe", "slab", None, None),
            P("probe", "slab", None, None),
        ),
        out_specs=(
            P("slab", "probe", None),
            P("slab", "probe", None),
            P("probe", "slab", None, None),
            P("probe", "slab", None, None),
        ),
        check_vma=False,
    )
```

```python
import functools

import numpy as np
import jax
import jax.numpy as jnp
from jax import lax
from jax.experimental import pallas as pl
from jax.experimental.pallas import tpu as pltpu
from jax.sharding import PartitionSpec as P


SECOND = (-205.0 / 72.0, 8.0 / 5.0, -1.0 / 5.0, 8.0 / 315.0, -1.0 / 560.0)
FIRST = (0.0, 4.0 / 5.0, -1.0 / 5.0, 4.0 / 105.0, -1.0 / 280.0)

BZ = 8
HALO = 4
INTERPRET = False
HI = lax.Precision.HIGHEST


def band_matrices(n):
    ms = np.zeros((n, n), np.float32)
    mg = np.zeros((n, n), np.float32)
    for i in range(n):
        for k in range(1, 5):
            for j, sign in ((i + k, 1.0), (i - k, -1.0)):
                if 0 <= j < n:
                    ms[i, j] = SECOND[k]
                    mg[i, j] = sign * FIRST[k]
    return ms, mg


def halo_depth(cells):
    count = lax.axis_size("slab")
    ends = count - 1
    head = cells[:HALO]
    tail = cells[cells.shape[0] - HALO:]
    return jnp.concatenate(
        [
            lax.ppermute(tail, "slab", [(i, i + 1) for i in range(ends)]),
            cells,
            lax.ppermute(head, "slab", [(i + 1, i) for i in range(ends)]),
        ],
        axis=0,
    )


def ring_gather(x):
    n = lax.axis_size("probe")
    rings = n // 2
    p = lax.axis_index("probe")
    partner = lax.ppermute(x, "probe", [(i, i ^ 1) for i in range(n)])
    pair = jnp.where(p % 2 == 0, jnp.concatenate([x, partner], 1), jnp.concatenate([partner, x], 1))
    ahead = [(i, (i + 2) % n) for i in range(n)]
    behind = [(i, (i - 2) % n) for i in range(n)]
    by_offset = {0: pair}
    fwd = pair
    bwd = pair
    half = rings // 2
    for k in range(1, half):
        fwd = lax.ppermute(fwd, "probe", ahead)
        bwd = lax.ppermute(bwd, "probe", behind)
        by_offset[-k % rings] = fwd
        by_offset[k] = bwd
    cut = x.shape[0] // 2
    far = jnp.concatenate(
        [lax.ppermute(fwd[:cut], "probe", ahead), lax.ppermute(bwd[cut:], "probe", behind)], axis=0
    )
    by_offset[half] = far
    ordered = jnp.concatenate([by_offset[d] for d in range(rings)] * 2, axis=1)
    width = pair.shape[1]
    start = ((rings - p // 2) % rings) * width
    return lax.dynamic_slice_in_dim(ordered, start, rings * width, 1)


def _ext(lo_ref, hi_ref, idx):
    if idx < BZ:
        return lo_ref[idx]
    return hi_ref[idx - BZ]


def _depth_terms(lo_ref, hi_ref, j):
    c = j + HALO
    centre = _ext(lo_ref, hi_ref, c)
    second = (3.0 * SECOND[0]) * centre
    grad = None
    for k in range(1, 5):
        up = _ext(lo_ref, hi_ref, c + k)
        down = _ext(lo_ref, hi_ref, c - k)
        second = second + SECOND[k] * (up + down)
        term = FIRST[k] * (up - down)
        grad = term if grad is None else grad + term
    return centre, second, grad


def _slope_kernel(lo_ref, hi_ref, mlane_ref, msub_ref, g0_ref, g1_ref, g2_ref):
    n = mlane_ref.shape[0]
    for j in range(BZ):
        centre, _, grad = _depth_terms(lo_ref, hi_ref, j)
        lane = jnp.dot(centre, mlane_ref[...], precision=HI, preferred_element_type=jnp.float32)
        sub = jnp.dot(msub_ref[...], centre, precision=HI, preferred_element_type=jnp.float32)
        g0_ref[j] = grad
        g1_ref[j] = sub[n:]
        g2_ref[j] = lane[:, n:]


def _op_kernel(flags, *refs):
    with_prev, with_img, want_image, want_step = flags
    refs = list(refs)
    lo_ref, hi_ref, b_ref, g0_ref, g1_ref, g2_ref, mlane_ref, msub_ref = refs[:8]
    rest = refs[8:]
    kappa_ref = prev_ref = dk_ref = img_ref = None
    if want_step:
        kappa_ref = rest.pop(0)
        if with_prev:
            prev_ref = rest.pop(0)
        if with_img:
            dk_ref = rest.pop(0)
            img_ref = rest.pop(0)
    outs = rest
    n = mlane_ref.shape[0]
    for j in range(BZ):
        centre, second, grad = _depth_terms(lo_ref, hi_ref, j)
        lane = jnp.dot(centre, mlane_ref[...], precision=HI, preferred_element_type=jnp.float32)
        sub = jnp.dot(msub_ref[...], centre, precision=HI, preferred_element_type=jnp.float32)
        second = second + sub[:n] + lane[:, :n]
        image = (
            b_ref[j] * second
            + g0_ref[j] * grad
            + g1_ref[j] * sub[n:]
            + g2_ref[j] * lane[:, n:]
        )
        at = 0
        if want_image:
            outs[at][j] = image
            at += 1
        if want_step:
            step = 2.0 * centre + kappa_ref[j] * image
            if with_prev:
                step = step - prev_ref[j]
            if with_img:
                step = step + dk_ref[j] * img_ref[j]
            outs[at][j] = step


def _specs(n, count):
    blk = pl.BlockSpec((BZ, n, n), lambda i: (i, 0, 0))
    return [blk] * count


def _ext_specs(n):
    return [
        pl.BlockSpec((BZ, n, n), lambda i: (i, 0, 0)),
        pl.BlockSpec((BZ, n, n), lambda i: (i + 1, 0, 0)),
    ]


def _mat_specs(n):
    return [
        pl.BlockSpec((n, 2 * n), lambda i: (0, 0)),
        pl.BlockSpec((2 * n, n), lambda i: (0, 0)),
    ]


def slopes_of(b_ext, mlane, msub):
    depth = b_ext.shape[0] - 2 * HALO
    n = b_ext.shape[1]
    shape = jax.ShapeDtypeStruct((depth, n, n), jnp.float32)
    return pl.pallas_call(
        _slope_kernel,
        grid=(depth // BZ,),
        in_specs=_ext_specs(n) + _mat_specs(n),
        out_specs=_specs(n, 3),
        out_shape=[shape] * 3,
        compiler_params=pltpu.CompilerParams(vmem_limit_bytes=48 * 1024 * 1024),
        interpret=INTERPRET,
    )(b_ext, b_ext, mlane, msub)


def apply_op(f_ext, b, slopes, mlane, msub, kappa=None, prev=None, dk=None, img=None, want_image=False):
    depth = f_ext.shape[0] - 2 * HALO
    n = f_ext.shape[1]
    want_step = kappa is not None
    with_prev = prev is not None
    with_img = img is not None
    args = [f_ext, f_ext, b, *slopes, mlane, msub]
    in_specs = _ext_specs(n) + _specs(n, 4) + _mat_specs(n)
    if want_step:
        extra = [kappa] + ([prev] if with_prev else []) + ([dk, img] if with_img else [])
        args += extra
        in_specs += _specs(n, len(extra))
    n_out = int(want_image) + int(want_step)
    shape = jax.ShapeDtypeStruct((depth, n, n), jnp.float32)
    outs = pl.pallas_call(
        functools.partial(_op_kernel, (with_prev, with_img, want_image, want_step)),
        grid=(depth // BZ,),
        in_specs=in_specs,
        out_specs=_specs(n, n_out),
        out_shape=[shape] * n_out,
        compiler_params=pltpu.CompilerParams(vmem_limit_bytes=48 * 1024 * 1024),
        interpret=INTERPRET,
    )(*args)
    return outs


def local_body(u_prev, u_cur, buoyancy, kappa, dkappa, du_prev, du_cur):
    n = buoyancy.shape[1]
    strip = u_cur.shape[1]
    offset = lax.axis_index("probe") * strip
    ms, mg = band_matrices(n)
    mlane = jnp.asarray(np.concatenate([ms, mg.T], axis=1))
    msub = jnp.asarray(np.concatenate([ms, mg], axis=0))

    depth = u_cur.shape[0]
    both = ring_gather(jnp.concatenate([halo_depth(u_cur), u_prev], axis=0))
    u_cur_ext = both[: depth + 2 * HALO]
    u_prev_all = both[depth + 2 * HALO:]

    buoyancy_ext = halo_depth(buoyancy)
    slopes = slopes_of(buoyancy_ext, mlane, msub)

    probe_kappa = dkappa[0]
    older = du_prev[0]
    newer = du_cur[0]

    newer_ext = halo_depth(newer)
    (partial_first,) = apply_op(newer_ext, buoyancy, slopes, mlane, msub, kappa=kappa, prev=older)

    image_first, background_first = apply_op(
        u_cur_ext, buoyancy, slopes, mlane, msub, kappa=kappa, prev=u_prev_all, want_image=True
    )
    born_first = partial_first + probe_kappa * image_first

    (image_second,) = apply_op(halo_depth(background_first), buoyancy, slopes, mlane, msub, want_image=True)

    def cut_strip(field):
        return lax.dynamic_slice_in_dim(field, offset, strip, 1)

    background_first_strip = cut_strip(background_first)
    background_second = (
        2.0 * background_first_strip - u_cur + cut_strip(kappa) * cut_strip(image_second)
    )

    (born_second,) = apply_op(
        halo_depth(born_first), buoyancy, slopes, mlane, msub,
        kappa=kappa, prev=newer, dk=probe_kappa, img=image_second,
    )
    return background_first_strip, background_second, born_first[None], born_second[None]


def solution(mesh):
    return shard_mapped(mesh)


def shard_mapped(mesh):
    return jax.shard_map(
        local_body,
        mesh=mesh,
        in_specs=(
            P("slab", "probe", None),
            P("slab", "probe", None),
            P("slab", None, None),
            P("slab", None, None),
            P("probe", "slab", None, None),
            P("probe", "slab", None, None),
            P("probe", "slab", None, None),
        ),
        out_specs=(
            P("slab", "probe", None),
            P("slab", "probe", None),
            P("probe", "slab", None, None),
            P("probe", "slab", None, None),
        ),
        check_vma=False,
    )
```

```python
import functools

import numpy as np
import jax
import jax.numpy as jnp
from jax import lax
from jax.experimental import pallas as pl
from jax.experimental.pallas import tpu as pltpu
from jax.sharding import PartitionSpec as P


SECOND = (-205.0 / 72.0, 8.0 / 5.0, -1.0 / 5.0, 8.0 / 315.0, -1.0 / 560.0)
FIRST = (0.0, 4.0 / 5.0, -1.0 / 5.0, 4.0 / 105.0, -1.0 / 280.0)

BZ = 8
HALO = 4
INTERPRET = False
HI = lax.Precision.HIGHEST


def band_matrices(n):
    ms = np.zeros((n, n), np.float32)
    mg = np.zeros((n, n), np.float32)
    for i in range(n):
        for k in range(1, 5):
            for j, sign in ((i + k, 1.0), (i - k, -1.0)):
                if 0 <= j < n:
                    ms[i, j] = SECOND[k]
                    mg[i, j] = sign * FIRST[k]
    return ms, mg


def halo_depth(cells):
    count = lax.axis_size("slab")
    ends = count - 1
    head = cells[:HALO]
    tail = cells[cells.shape[0] - HALO:]
    return jnp.concatenate(
        [
            lax.ppermute(tail, "slab", [(i, i + 1) for i in range(ends)]),
            cells,
            lax.ppermute(head, "slab", [(i + 1, i) for i in range(ends)]),
        ],
        axis=0,
    )


def ring_gather(x, bounds):
    n = lax.axis_size("probe")
    rings = n // 2
    p = lax.axis_index("probe")
    partner = lax.ppermute(x, "probe", [(i, i ^ 1) for i in range(n)])
    pair = jnp.where(p % 2 == 0, jnp.concatenate([x, partner], 1), jnp.concatenate([partner, x], 1))
    ahead = [(i, (i + 2) % n) for i in range(n)]
    behind = [(i, (i - 2) % n) for i in range(n)]
    by_offset = {0: pair}
    fwd = pair
    bwd = pair
    half = rings // 2
    for k in range(1, half):
        fwd = lax.ppermute(fwd, "probe", ahead)
        bwd = lax.ppermute(bwd, "probe", behind)
        by_offset[-k % rings] = fwd
        by_offset[k] = bwd
    cut = x.shape[0] // 2
    far = jnp.concatenate(
        [lax.ppermute(fwd[:cut], "probe", ahead), lax.ppermute(bwd[cut:], "probe", behind)], axis=0
    )
    by_offset[half] = far
    width = pair.shape[1]
    zpos = p // 2
    outs = []
    for lo, hi in bounds:
        buf = jnp.zeros((hi - lo, rings * width, x.shape[2]), x.dtype)
        for d in range(rings):
            at = ((zpos + d) % rings) * width
            buf = lax.dynamic_update_slice_in_dim(buf, by_offset[d][lo:hi], at, 1)
        outs.append(buf)
    return outs


def _ext(lo_ref, hi_ref, idx):
    if idx < BZ:
        return lo_ref[idx]
    return hi_ref[idx - BZ]


def _depth_terms(lo_ref, hi_ref, j):
    c = j + HALO
    centre = _ext(lo_ref, hi_ref, c)
    second = (3.0 * SECOND[0]) * centre
    grad = None
    for k in range(1, 5):
        up = _ext(lo_ref, hi_ref, c + k)
        down = _ext(lo_ref, hi_ref, c - k)
        second = second + SECOND[k] * (up + down)
        term = FIRST[k] * (up - down)
        grad = term if grad is None else grad + term
    return centre, second, grad


def _slope_kernel(lo_ref, hi_ref, mlane_ref, msub_ref, g0_ref, g1_ref, g2_ref):
    n = mlane_ref.shape[0]
    for j in range(BZ):
        centre, _, grad = _depth_terms(lo_ref, hi_ref, j)
        lane = jnp.dot(centre, mlane_ref[...], precision=HI, preferred_element_type=jnp.float32)
        sub = jnp.dot(msub_ref[...], centre, precision=HI, preferred_element_type=jnp.float32)
        g0_ref[j] = grad
        g1_ref[j] = sub[n:]
        g2_ref[j] = lane[:, n:]


def _op_kernel(flags, *refs):
    with_prev, with_img, want_image, want_step = flags
    refs = list(refs)
    lo_ref, hi_ref, b_ref, g0_ref, g1_ref, g2_ref, mlane_ref, msub_ref = refs[:8]
    rest = refs[8:]
    kappa_ref = prev_ref = dk_ref = img_ref = None
    if want_step:
        kappa_ref = rest.pop(0)
        if with_prev:
            prev_ref = rest.pop(0)
        if with_img:
            dk_ref = rest.pop(0)
            img_ref = rest.pop(0)
    outs = rest
    n = mlane_ref.shape[0]
    for j in range(BZ):
        centre, second, grad = _depth_terms(lo_ref, hi_ref, j)
        lane = jnp.dot(centre, mlane_ref[...], precision=HI, preferred_element_type=jnp.float32)
        sub = jnp.dot(msub_ref[...], centre, precision=HI, preferred_element_type=jnp.float32)
        second = second + sub[:n] + lane[:, :n]
        image = (
            b_ref[j] * second
            + g0_ref[j] * grad
            + g1_ref[j] * sub[n:]
            + g2_ref[j] * lane[:, n:]
        )
        at = 0
        if want_image:
            outs[at][j] = image
            at += 1
        if want_step:
            step = 2.0 * centre + kappa_ref[j] * image
            if with_prev:
                step = step - prev_ref[j]
            if with_img:
                step = step + dk_ref[j] * img_ref[j]
            outs[at][j] = step


def _specs(n, count):
    blk = pl.BlockSpec((BZ, n, n), lambda i: (i, 0, 0))
    return [blk] * count


def _ext_specs(n):
    return [
        pl.BlockSpec((BZ, n, n), lambda i: (i, 0, 0)),
        pl.BlockSpec((BZ, n, n), lambda i: (i + 1, 0, 0)),
    ]


def _mat_specs(n):
    return [
        pl.BlockSpec((n, 2 * n), lambda i: (0, 0)),
        pl.BlockSpec((2 * n, n), lambda i: (0, 0)),
    ]


def slopes_of(b_ext, mlane, msub):
    depth = b_ext.shape[0] - 2 * HALO
    n = b_ext.shape[1]
    shape = jax.ShapeDtypeStruct((depth, n, n), jnp.float32)
    return pl.pallas_call(
        _slope_kernel,
        grid=(depth // BZ,),
        in_specs=_ext_specs(n) + _mat_specs(n),
        out_specs=_specs(n, 3),
        out_shape=[shape] * 3,
        compiler_params=pltpu.CompilerParams(vmem_limit_bytes=48 * 1024 * 1024),
        interpret=INTERPRET,
    )(b_ext, b_ext, mlane, msub)


def apply_op(f_ext, b, slopes, mlane, msub, kappa=None, prev=None, dk=None, img=None, want_image=False):
    depth = f_ext.shape[0] - 2 * HALO
    n = f_ext.shape[1]
    want_step = kappa is not None
    with_prev = prev is not None
    with_img = img is not None
    args = [f_ext, f_ext, b, *slopes, mlane, msub]
    in_specs = _ext_specs(n) + _specs(n, 4) + _mat_specs(n)
    if want_step:
        extra = [kappa] + ([prev] if with_prev else []) + ([dk, img] if with_img else [])
        args += extra
        in_specs += _specs(n, len(extra))
    n_out = int(want_image) + int(want_step)
    shape = jax.ShapeDtypeStruct((depth, n, n), jnp.float32)
    outs = pl.pallas_call(
        functools.partial(_op_kernel, (with_prev, with_img, want_image, want_step)),
        grid=(depth // BZ,),
        in_specs=in_specs,
        out_specs=_specs(n, n_out),
        out_shape=[shape] * n_out,
        compiler_params=pltpu.CompilerParams(vmem_limit_bytes=48 * 1024 * 1024),
        interpret=INTERPRET,
    )(*args)
    return outs


def local_body(u_prev, u_cur, buoyancy, kappa, dkappa, du_prev, du_cur):
    n = buoyancy.shape[1]
    strip = u_cur.shape[1]
    offset = lax.axis_index("probe") * strip
    ms, mg = band_matrices(n)
    mlane = jnp.asarray(np.concatenate([ms, mg.T], axis=1))
    msub = jnp.asarray(np.concatenate([ms, mg], axis=0))

    depth = u_cur.shape[0]
    cur_rows = depth + 2 * HALO
    u_cur_ext, u_prev_all = ring_gather(
        jnp.concatenate([halo_depth(u_cur), u_prev], axis=0),
        ((0, cur_rows), (cur_rows, cur_rows + depth)),
    )

    buoyancy_ext = halo_depth(buoyancy)
    slopes = slopes_of(buoyancy_ext, mlane, msub)

    probe_kappa = dkappa[0]
    older = du_prev[0]
    newer = du_cur[0]

    newer_ext = halo_depth(newer)
    (partial_first,) = apply_op(newer_ext, buoyancy, slopes, mlane, msub, kappa=kappa, prev=older)

    image_first, background_first = apply_op(
        u_cur_ext, buoyancy, slopes, mlane, msub, kappa=kappa, prev=u_prev_all, want_image=True
    )
    born_first = partial_first + probe_kappa * image_first

    (image_second,) = apply_op(halo_depth(background_first), buoyancy, slopes, mlane, msub, want_image=True)

    def cut_strip(field):
        return lax.dynamic_slice_in_dim(field, offset, strip, 1)

    background_first_strip = cut_strip(background_first)
    background_second = (
        2.0 * background_first_strip - u_cur + cut_strip(kappa) * cut_strip(image_second)
    )

    (born_second,) = apply_op(
        halo_depth(born_first), buoyancy, slopes, mlane, msub,
        kappa=kappa, prev=newer, dk=probe_kappa, img=image_second,
    )
    return background_first_strip, background_second, born_first[None], born_second[None]


def solution(mesh):
    return shard_mapped(mesh)


def shard_mapped(mesh):
    return jax.shard_map(
        local_body,
        mesh=mesh,
        in_specs=(
            P("slab", "probe", None),
            P("slab", "probe", None),
            P("slab", None, None),
            P("slab", None, None),
            P("probe", "slab", None, None),
            P("probe", "slab", None, None),
            P("probe", "slab", None, None),
        ),
        out_specs=(
            P("slab", "probe", None),
            P("slab", "probe", None),
            P("probe", "slab", None, None),
            P("probe", "slab", None, None),
        ),
        check_vma=False,
    )
```

```python
import functools

import numpy as np
import jax
import jax.numpy as jnp
from jax import lax
from jax.experimental import pallas as pl
from jax.experimental.pallas import tpu as pltpu
from jax.sharding import PartitionSpec as P


SECOND = (-205.0 / 72.0, 8.0 / 5.0, -1.0 / 5.0, 8.0 / 315.0, -1.0 / 560.0)
FIRST = (0.0, 4.0 / 5.0, -1.0 / 5.0, 4.0 / 105.0, -1.0 / 280.0)

BZ = 8
HALO = 4
INTERPRET = False
HI = lax.Precision.HIGHEST


def band_matrices(n):
    ms = np.zeros((n, n), np.float32)
    mg = np.zeros((n, n), np.float32)
    for i in range(n):
        for k in range(1, 5):
            for j, sign in ((i + k, 1.0), (i - k, -1.0)):
                if 0 <= j < n:
                    ms[i, j] = SECOND[k]
                    mg[i, j] = sign * FIRST[k]
    return ms, mg


def halo_depth(cells):
    count = lax.axis_size("slab")
    ends = count - 1
    head = cells[:HALO]
    tail = cells[cells.shape[0] - HALO:]
    return jnp.concatenate(
        [
            lax.ppermute(tail, "slab", [(i, i + 1) for i in range(ends)]),
            cells,
            lax.ppermute(head, "slab", [(i + 1, i) for i in range(ends)]),
        ],
        axis=0,
    )


def ring_gather(x, bounds):
    n = lax.axis_size("probe")
    rings = n // 2
    p = lax.axis_index("probe")
    partner = lax.ppermute(x, "probe", [(i, i ^ 1) for i in range(n)])
    pair = jnp.where(p % 2 == 0, jnp.concatenate([x, partner], 1), jnp.concatenate([partner, x], 1))
    ahead = [(i, (i + 2) % n) for i in range(n)]
    behind = [(i, (i - 2) % n) for i in range(n)]
    by_offset = {0: pair}
    fwd = pair
    bwd = pair
    half = rings // 2
    for k in range(1, half):
        fwd = lax.ppermute(fwd, "probe", ahead)
        bwd = lax.ppermute(bwd, "probe", behind)
        by_offset[-k % rings] = fwd
        by_offset[k] = bwd
    cut = x.shape[0] // 2
    far = jnp.concatenate(
        [lax.ppermute(fwd[:cut], "probe", ahead), lax.ppermute(bwd[cut:], "probe", behind)], axis=0
    )
    by_offset[half] = far
    width = pair.shape[1]
    zpos = p // 2
    outs = []
    for lo, hi in bounds:
        buf = jnp.zeros((hi - lo, rings * width, x.shape[2]), x.dtype)
        for d in range(rings):
            at = ((zpos + d) % rings) * width
            buf = lax.dynamic_update_slice_in_dim(buf, by_offset[d][lo:hi], at, 1)
        outs.append(buf)
    return outs


def _ext(lo_ref, hi_ref, idx):
    if idx < BZ:
        return lo_ref[idx]
    return hi_ref[idx - BZ]


def _depth_terms(lo_ref, hi_ref, j, off, rows):
    c = j + HALO

    def at(idx):
        return _ext(lo_ref, hi_ref, idx)[off:off + rows]

    whole = _ext(lo_ref, hi_ref, c)
    centre = whole[off:off + rows]
    second = (3.0 * SECOND[0]) * centre
    grad = None
    for k in range(1, 5):
        up = at(c + k)
        down = at(c - k)
        second = second + SECOND[k] * (up + down)
        term = FIRST[k] * (up - down)
        grad = term if grad is None else grad + term
    return whole, centre, second, grad


def _slope_kernel(off, lo_ref, hi_ref, mlane_ref, msub_ref, g0_ref, g1_ref, g2_ref):
    n = mlane_ref.shape[0]
    rows = g0_ref.shape[1]
    for j in range(BZ):
        whole, centre, _, grad = _depth_terms(lo_ref, hi_ref, j, off, rows)
        lane = jnp.dot(centre, mlane_ref[...], precision=HI, preferred_element_type=jnp.float32)
        sub = jnp.dot(msub_ref[...], whole, precision=HI, preferred_element_type=jnp.float32)
        g0_ref[j] = grad
        g1_ref[j] = sub[rows:]
        g2_ref[j] = lane[:, n:]


def _op_kernel(flags, *refs):
    with_prev, with_img, want_image, want_step, off = flags
    refs = list(refs)
    lo_ref, hi_ref, b_ref, g0_ref, g1_ref, g2_ref, mlane_ref, msub_ref = refs[:8]
    rest = refs[8:]
    kappa_ref = prev_ref = dk_ref = img_ref = None
    if want_step:
        kappa_ref = rest.pop(0)
        if with_prev:
            prev_ref = rest.pop(0)
        if with_img:
            dk_ref = rest.pop(0)
            img_ref = rest.pop(0)
    outs = rest
    n = mlane_ref.shape[0]
    rows = b_ref.shape[1]
    for j in range(BZ):
        whole, centre, second, grad = _depth_terms(lo_ref, hi_ref, j, off, rows)
        lane = jnp.dot(centre, mlane_ref[...], precision=HI, preferred_element_type=jnp.float32)
        sub = jnp.dot(msub_ref[...], whole, precision=HI, preferred_element_type=jnp.float32)
        second = second + sub[:rows] + lane[:, :n]
        image = (
            b_ref[j] * second
            + g0_ref[j] * grad
            + g1_ref[j] * sub[rows:]
            + g2_ref[j] * lane[:, n:]
        )
        at = 0
        if want_image:
            outs[at][j] = image
            at += 1
        if want_step:
            step = 2.0 * centre + kappa_ref[j] * image
            if with_prev:
                step = step - prev_ref[j]
            if with_img:
                step = step + dk_ref[j] * img_ref[j]
            outs[at][j] = step


def _specs(rows, n, count):
    blk = pl.BlockSpec((BZ, rows, n), lambda i: (i, 0, 0))
    return [blk] * count


def _ext_specs(rows, n):
    return [
        pl.BlockSpec((BZ, rows, n), lambda i: (i, 0, 0)),
        pl.BlockSpec((BZ, rows, n), lambda i: (i + 1, 0, 0)),
    ]


def _mat_specs(mlane, msub):
    return [
        pl.BlockSpec(mlane.shape, lambda i: (0, 0)),
        pl.BlockSpec(msub.shape, lambda i: (0, 0)),
    ]


PARAMS = pltpu.CompilerParams(vmem_limit_bytes=48 * 1024 * 1024)


def slopes_of(b_ext, mlane, msub):
    depth = b_ext.shape[0] - 2 * HALO
    rows_in = b_ext.shape[1]
    rows = msub.shape[0] // 2
    n = b_ext.shape[2]
    shape = jax.ShapeDtypeStruct((depth, rows, n), jnp.float32)
    return pl.pallas_call(
        functools.partial(_slope_kernel, (rows_in - rows) // 2),
        grid=(depth // BZ,),
        in_specs=_ext_specs(rows_in, n) + _mat_specs(mlane, msub),
        out_specs=_specs(rows, n, 3),
        out_shape=[shape] * 3,
        compiler_params=PARAMS,
        interpret=INTERPRET,
    )(b_ext, b_ext, mlane, msub)


def apply_op(f_ext, b, slopes, mlane, msub, kappa=None, prev=None, dk=None, img=None, want_image=False):
    depth = f_ext.shape[0] - 2 * HALO
    rows_in = f_ext.shape[1]
    rows = b.shape[1]
    n = f_ext.shape[2]
    off = (rows_in - rows) // 2
    want_step = kappa is not None
    with_prev = prev is not None
    with_img = img is not None
    args = [f_ext, f_ext, b, *slopes, mlane, msub]
    in_specs = _ext_specs(rows_in, n) + _specs(rows, n, 4) + _mat_specs(mlane, msub)
    if want_step:
        extra = [kappa] + ([prev] if with_prev else []) + ([dk, img] if with_img else [])
        args += extra
        in_specs += _specs(rows, n, len(extra))
    n_out = int(want_image) + int(want_step)
    shape = jax.ShapeDtypeStruct((depth, rows, n), jnp.float32)
    outs = pl.pallas_call(
        functools.partial(_op_kernel, (with_prev, with_img, want_image, want_step, off)),
        grid=(depth // BZ,),
        in_specs=in_specs,
        out_specs=_specs(rows, n, n_out),
        out_shape=[shape] * n_out,
        compiler_params=PARAMS,
        interpret=INTERPRET,
    )(*args)
    return outs


def halo_rows(cells):
    count = lax.axis_size("probe")
    ends = count - 1
    head = cells[:, :HALO]
    tail = cells[:, cells.shape[1] - HALO:]
    return jnp.concatenate(
        [
            lax.ppermute(tail, "probe", [(i, i + 1) for i in range(ends)]),
            cells,
            lax.ppermute(head, "probe", [(i + 1, i) for i in range(ends)]),
        ],
        axis=1,
    )


def local_body(u_prev, u_cur, buoyancy, kappa, dkappa, du_prev, du_cur):
    n = buoyancy.shape[1]
    strip = u_cur.shape[1]
    offset = lax.axis_index("probe") * strip
    ms, mg = band_matrices(n)
    mlane = jnp.asarray(np.concatenate([ms, mg.T], axis=1))
    msub = jnp.asarray(np.concatenate([ms, mg], axis=0))
    rows_in = strip + 2 * HALO
    ms_s, mg_s = band_matrices(rows_in)
    msub_strip = jnp.asarray(np.concatenate([ms_s[HALO:HALO + strip], mg_s[HALO:HALO + strip]], axis=0))

    buoyancy_ext = halo_depth(buoyancy)
    slopes = slopes_of(buoyancy_ext, mlane, msub)

    def cut_strip(field):
        return lax.dynamic_slice_in_dim(field, offset, strip, 1)

    strip_b = cut_strip(buoyancy)
    rimmed = jnp.pad(buoyancy_ext, [(0, 0), (HALO, HALO), (0, 0)])
    strip_slopes = slopes_of(lax.dynamic_slice_in_dim(rimmed, offset, rows_in, 1), mlane, msub_strip)
    strip_kappa = cut_strip(kappa)

    image_first_strip, background_first = apply_op(
        halo_rows(halo_depth(u_cur)), strip_b, strip_slopes, mlane, msub_strip,
        kappa=strip_kappa, prev=u_prev, want_image=True,
    )
    (image_first,) = ring_gather(image_first_strip, ((0, image_first_strip.shape[0]),))
    (image_second_strip,) = apply_op(
        halo_rows(halo_depth(background_first)), strip_b, strip_slopes, mlane, msub_strip,
        want_image=True,
    )
    background_second = 2.0 * background_first - u_cur + strip_kappa * image_second_strip
    (image_second,) = ring_gather(image_second_strip, ((0, image_second_strip.shape[0]),))

    probe_kappa = dkappa[0]
    older = du_prev[0]
    newer = du_cur[0]
    newer_ext = halo_depth(newer)
    (partial_first,) = apply_op(newer_ext, buoyancy, slopes, mlane, msub, kappa=kappa, prev=older)
    born_first = partial_first + probe_kappa * image_first
    (partial_second,) = apply_op(
        halo_depth(born_first), buoyancy, slopes, mlane, msub, kappa=kappa, prev=newer
    )
    born_second = partial_second + probe_kappa * image_second
    return background_first, background_second, born_first[None], born_second[None]


def solution(mesh):
    return shard_mapped(mesh)


def shard_mapped(mesh):
    return jax.shard_map(
        local_body,
        mesh=mesh,
        in_specs=(
            P("slab", "probe", None),
            P("slab", "probe", None),
            P("slab", None, None),
            P("slab", None, None),
            P("probe", "slab", None, None),
            P("probe", "slab", None, None),
            P("probe", "slab", None, None),
        ),
        out_specs=(
            P("slab", "probe", None),
            P("slab", "probe", None),
            P("probe", "slab", None, None),
            P("probe", "slab", None, None),
        ),
        check_vma=False,
    )
```

```python
import functools

import numpy as np
import jax
import jax.numpy as jnp
from jax import lax
from jax.experimental import pallas as pl
from jax.experimental.pallas import tpu as pltpu
from jax.sharding import PartitionSpec as P


SECOND = (-205.0 / 72.0, 8.0 / 5.0, -1.0 / 5.0, 8.0 / 315.0, -1.0 / 560.0)
FIRST = (0.0, 4.0 / 5.0, -1.0 / 5.0, 4.0 / 105.0, -1.0 / 280.0)

BZ = 8
HALO = 4
INTERPRET = False
HI = lax.Precision.HIGHEST


def band_matrices(n):
    ms = np.zeros((n, n), np.float32)
    mg = np.zeros((n, n), np.float32)
    for i in range(n):
        for k in range(1, 5):
            for j, sign in ((i + k, 1.0), (i - k, -1.0)):
                if 0 <= j < n:
                    ms[i, j] = SECOND[k]
                    mg[i, j] = sign * FIRST[k]
    return ms, mg


def halo_depth_many(fields):
    count = lax.axis_size("slab")
    ends = count - 1
    heads = jnp.concatenate([f[:HALO] for f in fields], axis=1)
    tails = jnp.concatenate([f[f.shape[0] - HALO:] for f in fields], axis=1)
    above = lax.ppermute(tails, "slab", [(i, i + 1) for i in range(ends)])
    below = lax.ppermute(heads, "slab", [(i + 1, i) for i in range(ends)])
    outs = []
    at = 0
    for f in fields:
        w = f.shape[1]
        outs.append(jnp.concatenate([above[:, at:at + w], f, below[:, at:at + w]], axis=0))
        at += w
    return outs


def ring_gather(x, bounds):
    n = lax.axis_size("probe")
    rings = n // 2
    p = lax.axis_index("probe")
    partner = lax.ppermute(x, "probe", [(i, i ^ 1) for i in range(n)])
    pair = jnp.where(p % 2 == 0, jnp.concatenate([x, partner], 1), jnp.concatenate([partner, x], 1))
    ahead = [(i, (i + 2) % n) for i in range(n)]
    behind = [(i, (i - 2) % n) for i in range(n)]
    by_offset = {0: pair}
    fwd = pair
    bwd = pair
    half = rings // 2
    for k in range(1, half):
        fwd = lax.ppermute(fwd, "probe", ahead)
        bwd = lax.ppermute(bwd, "probe", behind)
        by_offset[-k % rings] = fwd
        by_offset[k] = bwd
    cut = x.shape[0] // 2
    far = jnp.concatenate(
        [lax.ppermute(fwd[:cut], "probe", ahead), lax.ppermute(bwd[cut:], "probe", behind)], axis=0
    )
    by_offset[half] = far
    width = pair.shape[1]
    zpos = p // 2
    outs = []
    for lo, hi in bounds:
        buf = jnp.zeros((hi - lo, rings * width, x.shape[2]), x.dtype)
        for d in range(rings):
            at = ((zpos + d) % rings) * width
            buf = lax.dynamic_update_slice_in_dim(buf, by_offset[d][lo:hi], at, 1)
        outs.append(buf)
    return outs


def _ext(lo_ref, hi_ref, idx):
    if idx < BZ:
        return lo_ref[idx]
    return hi_ref[idx - BZ]


def _depth_terms(lo_ref, hi_ref, j):
    c = j + HALO
    centre = _ext(lo_ref, hi_ref, c)
    second = (3.0 * SECOND[0]) * centre
    grad = None
    for k in range(1, 5):
        up = _ext(lo_ref, hi_ref, c + k)
        down = _ext(lo_ref, hi_ref, c - k)
        second = second + SECOND[k] * (up + down)
        term = FIRST[k] * (up - down)
        grad = term if grad is None else grad + term
    return centre, second, grad


def _slope_kernel(lo_ref, hi_ref, mlane_ref, msub_ref, g0_ref, g1_ref, g2_ref):
    n = mlane_ref.shape[0]
    for j in range(BZ):
        centre, _, grad = _depth_terms(lo_ref, hi_ref, j)
        lane = jnp.dot(centre, mlane_ref[...], precision=HI, preferred_element_type=jnp.float32)
        sub = jnp.dot(msub_ref[...], centre, precision=HI, preferred_element_type=jnp.float32)
        g0_ref[j] = grad
        g1_ref[j] = sub[n:]
        g2_ref[j] = lane[:, n:]


def _op_kernel(flags, *refs):
    with_prev, with_img, want_image, want_step = flags
    refs = list(refs)
    lo_ref, hi_ref, b_ref, g0_ref, g1_ref, g2_ref, mlane_ref, msub_ref = refs[:8]
    rest = refs[8:]
    kappa_ref = prev_ref = dk_ref = img_ref = None
    if want_step:
        kappa_ref = rest.pop(0)
        if with_prev:
            prev_ref = rest.pop(0)
        if with_img:
            dk_ref = rest.pop(0)
            img_ref = rest.pop(0)
    outs = rest
    n = mlane_ref.shape[0]
    for j in range(BZ):
        centre, second, grad = _depth_terms(lo_ref, hi_ref, j)
        lane = jnp.dot(centre, mlane_ref[...], precision=HI, preferred_element_type=jnp.float32)
        sub = jnp.dot(msub_ref[...], centre, precision=HI, preferred_element_type=jnp.float32)
        second = second + sub[:n] + lane[:, :n]
        image = (
            b_ref[j] * second
            + g0_ref[j] * grad
            + g1_ref[j] * sub[n:]
            + g2_ref[j] * lane[:, n:]
        )
        at = 0
        if want_image:
            outs[at][j] = image
            at += 1
        if want_step:
            step = 2.0 * centre + kappa_ref[j] * image
            if with_prev:
                step = step - prev_ref[j]
            if with_img:
                step = step + dk_ref[j] * img_ref[j]
            outs[at][j] = step


def _specs(n, count):
    blk = pl.BlockSpec((BZ, n, n), lambda i: (i, 0, 0))
    return [blk] * count


def _ext_specs(n):
    return [
        pl.BlockSpec((BZ, n, n), lambda i: (i, 0, 0)),
        pl.BlockSpec((BZ, n, n), lambda i: (i + 1, 0, 0)),
    ]


def _mat_specs(n):
    return [
        pl.BlockSpec((n, 2 * n), lambda i: (0, 0)),
        pl.BlockSpec((2 * n, n), lambda i: (0, 0)),
    ]


def slopes_of(b_ext, mlane, msub):
    depth = b_ext.shape[0] - 2 * HALO
    n = b_ext.shape[1]
    shape = jax.ShapeDtypeStruct((depth, n, n), jnp.float32)
    return pl.pallas_call(
        _slope_kernel,
        grid=(depth // BZ,),
        in_specs=_ext_specs(n) + _mat_specs(n),
        out_specs=_specs(n, 3),
        out_shape=[shape] * 3,
        compiler_params=pltpu.CompilerParams(vmem_limit_bytes=48 * 1024 * 1024),
        interpret=INTERPRET,
    )(b_ext, b_ext, mlane, msub)


def apply_op(f_ext, b, slopes, mlane, msub, kappa=None, prev=None, dk=None, img=None, want_image=False):
    depth = f_ext.shape[0] - 2 * HALO
    n = f_ext.shape[1]
    want_step = kappa is not None
    with_prev = prev is not None
    with_img = img is not None
    args = [f_ext, f_ext, b, *slopes, mlane, msub]
    in_specs = _ext_specs(n) + _specs(n, 4) + _mat_specs(n)
    if want_step:
        extra = [kappa] + ([prev] if with_prev else []) + ([dk, img] if with_img else [])
        args += extra
        in_specs += _specs(n, len(extra))
    n_out = int(want_image) + int(want_step)
    shape = jax.ShapeDtypeStruct((depth, n, n), jnp.float32)
    outs = pl.pallas_call(
        functools.partial(_op_kernel, (with_prev, with_img, want_image, want_step)),
        grid=(depth // BZ,),
        in_specs=in_specs,
        out_specs=_specs(n, n_out),
        out_shape=[shape] * n_out,
        compiler_params=pltpu.CompilerParams(vmem_limit_bytes=48 * 1024 * 1024),
        interpret=INTERPRET,
    )(*args)
    return outs


def local_body(u_prev, u_cur, buoyancy, kappa, dkappa, du_prev, du_cur):
    n = buoyancy.shape[1]
    strip = u_cur.shape[1]
    offset = lax.axis_index("probe") * strip
    ms, mg = band_matrices(n)
    mlane = jnp.asarray(np.concatenate([ms, mg.T], axis=1))
    msub = jnp.asarray(np.concatenate([ms, mg], axis=0))

    depth = u_cur.shape[0]
    cur_rows = depth + 2 * HALO
    probe_kappa = dkappa[0]
    older = du_prev[0]
    newer = du_cur[0]
    u_cur_strip_ext, buoyancy_ext, newer_ext = halo_depth_many([u_cur, buoyancy, newer])
    u_cur_ext, u_prev_all = ring_gather(
        jnp.concatenate([u_cur_strip_ext, u_prev], axis=0),
        ((0, cur_rows), (cur_rows, cur_rows + depth)),
    )

    slopes = slopes_of(buoyancy_ext, mlane, msub)

    (partial_first,) = apply_op(newer_ext, buoyancy, slopes, mlane, msub, kappa=kappa, prev=older)

    image_first, background_first = apply_op(
        u_cur_ext, buoyancy, slopes, mlane, msub, kappa=kappa, prev=u_prev_all, want_image=True
    )
    born_first = partial_first + probe_kappa * image_first

    background_first_ext, born_first_ext = halo_depth_many([background_first, born_first])
    (image_second,) = apply_op(background_first_ext, buoyancy, slopes, mlane, msub, want_image=True)

    def cut_strip(field):
        return lax.dynamic_slice_in_dim(field, offset, strip, 1)

    background_first_strip = cut_strip(background_first)
    background_second = (
        2.0 * background_first_strip - u_cur + cut_strip(kappa) * cut_strip(image_second)
    )

    (born_second,) = apply_op(
        born_first_ext, buoyancy, slopes, mlane, msub,
        kappa=kappa, prev=newer, dk=probe_kappa, img=image_second,
    )
    return background_first_strip, background_second, born_first[None], born_second[None]


def solution(mesh):
    return shard_mapped(mesh)


def shard_mapped(mesh):
    return jax.shard_map(
        local_body,
        mesh=mesh,
        in_specs=(
            P("slab", "probe", None),
            P("slab", "probe", None),
            P("slab", None, None),
            P("slab", None, None),
            P("probe", "slab", None, None),
            P("probe", "slab", None, None),
            P("probe", "slab", None, None),
        ),
        out_specs=(
            P("slab", "probe", None),
            P("slab", "probe", None),
            P("probe", "slab", None, None),
            P("probe", "slab", None, None),
        ),
        check_vma=False,
    )
```

```python
import functools

import numpy as np
import jax
import jax.numpy as jnp
from jax import lax
from jax.experimental import pallas as pl
from jax.experimental.pallas import tpu as pltpu
from jax.sharding import PartitionSpec as P


SECOND = (-205.0 / 72.0, 8.0 / 5.0, -1.0 / 5.0, 8.0 / 315.0, -1.0 / 560.0)
FIRST = (0.0, 4.0 / 5.0, -1.0 / 5.0, 4.0 / 105.0, -1.0 / 280.0)

BZ = 8
HALO = 4
INTERPRET = False
HI = lax.Precision.HIGHEST


def band_matrices(n):
    ms = np.zeros((n, n), np.float32)
    mg = np.zeros((n, n), np.float32)
    for i in range(n):
        for k in range(1, 5):
            for j, sign in ((i + k, 1.0), (i - k, -1.0)):
                if 0 <= j < n:
                    ms[i, j] = SECOND[k]
                    mg[i, j] = sign * FIRST[k]
    return ms, mg


def halo_depth_many(fields):
    count = lax.axis_size("slab")
    ends = count - 1
    heads = jnp.concatenate([f[:HALO] for f in fields], axis=1)
    tails = jnp.concatenate([f[f.shape[0] - HALO:] for f in fields], axis=1)
    above = lax.ppermute(tails, "slab", [(i, i + 1) for i in range(ends)])
    below = lax.ppermute(heads, "slab", [(i + 1, i) for i in range(ends)])
    outs = []
    at = 0
    for f in fields:
        w = f.shape[1]
        outs.append(jnp.concatenate([above[:, at:at + w], f, below[:, at:at + w]], axis=0))
        at += w
    return outs


def ring_gather(x, bounds):
    n = lax.axis_size("probe")
    rings = n // 2
    p = lax.axis_index("probe")
    partner = lax.ppermute(x, "probe", [(i, i ^ 1) for i in range(n)])
    pair = jnp.where(p % 2 == 0, jnp.concatenate([x, partner], 1), jnp.concatenate([partner, x], 1))
    ahead = [(i, (i + 2) % n) for i in range(n)]
    behind = [(i, (i - 2) % n) for i in range(n)]
    by_offset = {0: pair}
    fwd = pair
    bwd = pair
    half = rings // 2
    for k in range(1, half):
        fwd = lax.ppermute(fwd, "probe", ahead)
        bwd = lax.ppermute(bwd, "probe", behind)
        by_offset[-k % rings] = fwd
        by_offset[k] = bwd
    cut = x.shape[0] // 2
    far = jnp.concatenate(
        [lax.ppermute(fwd[:cut], "probe", ahead), lax.ppermute(bwd[cut:], "probe", behind)], axis=0
    )
    by_offset[half] = far
    width = pair.shape[1]
    zpos = p // 2
    outs = []
    for lo, hi in bounds:
        buf = jnp.zeros((hi - lo, rings * width, x.shape[2]), x.dtype)
        for d in range(rings):
            at = ((zpos + d) % rings) * width
            buf = lax.dynamic_update_slice_in_dim(buf, by_offset[d][lo:hi], at, 1)
        outs.append(buf)
    return outs


def _ext(lo_ref, hi_ref, idx):
    if idx < BZ:
        return lo_ref[idx]
    return hi_ref[idx - BZ]


def _depth_terms(lo_ref, hi_ref, j, off, rows):
    c = j + HALO

    def at(idx):
        return _ext(lo_ref, hi_ref, idx)[off:off + rows]

    whole = _ext(lo_ref, hi_ref, c)
    centre = whole[off:off + rows]
    second = (3.0 * SECOND[0]) * centre
    grad = None
    for k in range(1, 5):
        up = at(c + k)
        down = at(c - k)
        second = second + SECOND[k] * (up + down)
        term = FIRST[k] * (up - down)
        grad = term if grad is None else grad + term
    return whole, centre, second, grad


def _slope_kernel(off, lo_ref, hi_ref, mlane_ref, msub_ref, g0_ref, g1_ref, g2_ref):
    n = mlane_ref.shape[0]
    rows = g0_ref.shape[1]
    for j in range(BZ):
        whole, centre, _, grad = _depth_terms(lo_ref, hi_ref, j, off, rows)
        lane = jnp.dot(centre, mlane_ref[...], precision=HI, preferred_element_type=jnp.float32)
        sub = jnp.dot(msub_ref[...], whole, precision=HI, preferred_element_type=jnp.float32)
        g0_ref[j] = grad
        g1_ref[j] = sub[rows:]
        g2_ref[j] = lane[:, n:]


def _image_of(lo_ref, hi_ref, j, coef, mlane_ref, msub_ref, off, rows):
    b_ref, g0_ref, g1_ref, g2_ref = coef
    n = mlane_ref.shape[0]
    whole, centre, second, grad = _depth_terms(lo_ref, hi_ref, j, off, rows)
    lane = jnp.dot(centre, mlane_ref[...], precision=HI, preferred_element_type=jnp.float32)
    sub = jnp.dot(msub_ref[...], whole, precision=HI, preferred_element_type=jnp.float32)
    second = second + sub[:rows] + lane[:, :n]
    image = (
        b_ref[j] * second
        + g0_ref[j] * grad
        + g1_ref[j] * sub[rows:]
        + g2_ref[j] * lane[:, n:]
    )
    return centre, image


def _op_kernel(flags, *refs):
    with_prev, with_img, want_image, want_step, off = flags
    refs = list(refs)
    lo_ref, hi_ref, b_ref, g0_ref, g1_ref, g2_ref, mlane_ref, msub_ref = refs[:8]
    rest = refs[8:]
    kappa_ref = prev_ref = dk_ref = img_ref = None
    if want_step:
        kappa_ref = rest.pop(0)
        if with_prev:
            prev_ref = rest.pop(0)
        if with_img:
            dk_ref = rest.pop(0)
            img_ref = rest.pop(0)
    outs = rest
    rows = b_ref.shape[1]
    coef = (b_ref, g0_ref, g1_ref, g2_ref)
    for j in range(BZ):
        centre, image = _image_of(lo_ref, hi_ref, j, coef, mlane_ref, msub_ref, off, rows)
        at = 0
        if want_image:
            outs[at][j] = image
            at += 1
        if want_step:
            step = 2.0 * centre + kappa_ref[j] * image
            if with_prev:
                step = step - prev_ref[j]
            if with_img:
                step = step + dk_ref[j] * img_ref[j]
            outs[at][j] = step


def _first_kernel(lo_ref, hi_ref, b_ref, g0_ref, g1_ref, g2_ref, mlane_ref, msub_ref,
                  kappa_ref, prev_ref, part_ref, dk_ref, bg_ref, born_ref):
    rows = b_ref.shape[1]
    coef = (b_ref, g0_ref, g1_ref, g2_ref)
    for j in range(BZ):
        centre, image = _image_of(lo_ref, hi_ref, j, coef, mlane_ref, msub_ref, 0, rows)
        bg_ref[j] = 2.0 * centre - prev_ref[j] + kappa_ref[j] * image
        born_ref[j] = part_ref[j] + dk_ref[j] * image


def _second_kernel(lo1_ref, hi1_ref, lo2_ref, hi2_ref, b_ref, g0_ref, g1_ref, g2_ref,
                   mlane_ref, msub_ref, kappa_ref, prev_ref, dk_ref, img_ref, born_ref):
    rows = b_ref.shape[1]
    coef = (b_ref, g0_ref, g1_ref, g2_ref)
    for j in range(BZ):
        _, image = _image_of(lo1_ref, hi1_ref, j, coef, mlane_ref, msub_ref, 0, rows)
        img_ref[j] = image
        centre, own = _image_of(lo2_ref, hi2_ref, j, coef, mlane_ref, msub_ref, 0, rows)
        born_ref[j] = 2.0 * centre - prev_ref[j] + kappa_ref[j] * own + dk_ref[j] * image


def _specs(rows, n, count):
    blk = pl.BlockSpec((BZ, rows, n), lambda i: (i, 0, 0))
    return [blk] * count


def _ext_specs(rows, n):
    return [
        pl.BlockSpec((BZ, rows, n), lambda i: (i, 0, 0)),
        pl.BlockSpec((BZ, rows, n), lambda i: (i + 1, 0, 0)),
    ]


def _mat_specs(mlane, msub):
    return [
        pl.BlockSpec(mlane.shape, lambda i: (0, 0)),
        pl.BlockSpec(msub.shape, lambda i: (0, 0)),
    ]


PARAMS = pltpu.CompilerParams(vmem_limit_bytes=48 * 1024 * 1024)


def slopes_of(b_ext, mlane, msub):
    depth = b_ext.shape[0] - 2 * HALO
    rows_in = b_ext.shape[1]
    rows = msub.shape[0] // 2
    n = b_ext.shape[2]
    shape = jax.ShapeDtypeStruct((depth, rows, n), jnp.float32)
    return pl.pallas_call(
        functools.partial(_slope_kernel, (rows_in - rows) // 2),
        grid=(depth // BZ,),
        in_specs=_ext_specs(rows_in, n) + _mat_specs(mlane, msub),
        out_specs=_specs(rows, n, 3),
        out_shape=[shape] * 3,
        compiler_params=PARAMS,
        interpret=INTERPRET,
    )(b_ext, b_ext, mlane, msub)


def apply_op(f_ext, b, slopes, mlane, msub, kappa=None, prev=None, dk=None, img=None, want_image=False):
    depth = f_ext.shape[0] - 2 * HALO
    rows_in = f_ext.shape[1]
    rows = b.shape[1]
    n = f_ext.shape[2]
    off = (rows_in - rows) // 2
    want_step = kappa is not None
    with_prev = prev is not None
    with_img = img is not None
    args = [f_ext, f_ext, b, *slopes, mlane, msub]
    in_specs = _ext_specs(rows_in, n) + _specs(rows, n, 4) + _mat_specs(mlane, msub)
    if want_step:
        extra = [kappa] + ([prev] if with_prev else []) + ([dk, img] if with_img else [])
        args += extra
        in_specs += _specs(rows, n, len(extra))
    n_out = int(want_image) + int(want_step)
    shape = jax.ShapeDtypeStruct((depth, rows, n), jnp.float32)
    outs = pl.pallas_call(
        functools.partial(_op_kernel, (with_prev, with_img, want_image, want_step, off)),
        grid=(depth // BZ,),
        in_specs=in_specs,
        out_specs=_specs(rows, n, n_out),
        out_shape=[shape] * n_out,
        compiler_params=PARAMS,
        interpret=INTERPRET,
    )(*args)
    return outs


def first_step(u_cur_ext, b, slopes, mlane, msub, kappa, u_prev, partial, dk):
    depth = u_cur_ext.shape[0] - 2 * HALO
    n = u_cur_ext.shape[2]
    shape = jax.ShapeDtypeStruct((depth, n, n), jnp.float32)
    return pl.pallas_call(
        _first_kernel,
        grid=(depth // BZ,),
        in_specs=_ext_specs(n, n) + _specs(n, n, 4) + _mat_specs(mlane, msub) + _specs(n, n, 4),
        out_specs=_specs(n, n, 2),
        out_shape=[shape] * 2,
        compiler_params=PARAMS,
        interpret=INTERPRET,
    )(u_cur_ext, u_cur_ext, b, *slopes, mlane, msub, kappa, u_prev, partial, dk)


def second_step(bg_ext, born_ext, b, slopes, mlane, msub, kappa, prev, dk):
    depth = bg_ext.shape[0] - 2 * HALO
    n = bg_ext.shape[2]
    shape = jax.ShapeDtypeStruct((depth, n, n), jnp.float32)
    return pl.pallas_call(
        _second_kernel,
        grid=(depth // BZ,),
        in_specs=_ext_specs(n, n) * 2 + _specs(n, n, 4) + _mat_specs(mlane, msub) + _specs(n, n, 3),
        out_specs=_specs(n, n, 2),
        out_shape=[shape] * 2,
        compiler_params=PARAMS,
        interpret=INTERPRET,
    )(bg_ext, bg_ext, born_ext, born_ext, b, *slopes, mlane, msub, kappa, prev, dk)


def local_body(u_prev, u_cur, buoyancy, kappa, dkappa, du_prev, du_cur):
    n = buoyancy.shape[1]
    strip = u_cur.shape[1]
    offset = lax.axis_index("probe") * strip
    ms, mg = band_matrices(n)
    mlane = jnp.asarray(np.concatenate([ms, mg.T], axis=1))
    msub = jnp.asarray(np.concatenate([ms, mg], axis=0))

    depth = u_cur.shape[0]
    cur_rows = depth + 2 * HALO
    probe_kappa = dkappa[0]
    older = du_prev[0]
    newer = du_cur[0]
    u_cur_strip_ext, buoyancy_ext, newer_ext = halo_depth_many([u_cur, buoyancy, newer])
    u_cur_ext, u_prev_all = ring_gather(
        jnp.concatenate([u_cur_strip_ext, u_prev], axis=0),
        ((0, cur_rows), (cur_rows, cur_rows + depth)),
    )

    slopes = slopes_of(buoyancy_ext, mlane, msub)

    (partial_first,) = apply_op(newer_ext, buoyancy, slopes, mlane, msub, kappa=kappa, prev=older)

    background_first, born_first = first_step(
        u_cur_ext, buoyancy, slopes, mlane, msub, kappa, u_prev_all, partial_first, probe_kappa
    )

    background_first_ext, born_first_ext = halo_depth_many([background_first, born_first])
    image_second, born_second = second_step(
        background_first_ext, born_first_ext, buoyancy, slopes, mlane, msub, kappa, newer, probe_kappa
    )

    def cut_strip(field):
        return lax.dynamic_slice_in_dim(field, offset, strip, 1)

    background_first_strip = cut_strip(background_first)
    background_second = (
        2.0 * background_first_strip - u_cur + cut_strip(kappa) * cut_strip(image_second)
    )
    return background_first_strip, background_second, born_first[None], born_second[None]


def solution(mesh):
    return shard_mapped(mesh)


def shard_mapped(mesh):
    return jax.shard_map(
        local_body,
        mesh=mesh,
        in_specs=(
            P("slab", "probe", None),
            P("slab", "probe", None),
            P("slab", None, None),
            P("slab", None, None),
            P("probe", "slab", None, None),
            P("probe", "slab", None, None),
            P("probe", "slab", None, None),
        ),
        out_specs=(
            P("slab", "probe", None),
            P("slab", "probe", None),
            P("probe", "slab", None, None),
            P("probe", "slab", None, None),
        ),
        check_vma=False,
    )
```

```python
import functools

import numpy as np
import jax
import jax.numpy as jnp
from jax import lax
from jax.experimental import pallas as pl
from jax.experimental.pallas import tpu as pltpu
from jax.sharding import PartitionSpec as P


SECOND = (-205.0 / 72.0, 8.0 / 5.0, -1.0 / 5.0, 8.0 / 315.0, -1.0 / 560.0)
FIRST = (0.0, 4.0 / 5.0, -1.0 / 5.0, 4.0 / 105.0, -1.0 / 280.0)

BZ = 8
HALO = 4
INTERPRET = False
HI = lax.Precision.HIGHEST


def band_matrices(n):
    ms = np.zeros((n, n), np.float32)
    mg = np.zeros((n, n), np.float32)
    for i in range(n):
        for k in range(1, 5):
            for j, sign in ((i + k, 1.0), (i - k, -1.0)):
                if 0 <= j < n:
                    ms[i, j] = SECOND[k]
                    mg[i, j] = sign * FIRST[k]
    return ms, mg


def halo_depth_many(fields):
    count = lax.axis_size("slab")
    ends = count - 1
    heads = jnp.concatenate([f[:HALO] for f in fields], axis=1)
    tails = jnp.concatenate([f[f.shape[0] - HALO:] for f in fields], axis=1)
    above = lax.ppermute(tails, "slab", [(i, i + 1) for i in range(ends)])
    below = lax.ppermute(heads, "slab", [(i + 1, i) for i in range(ends)])
    outs = []
    at = 0
    for f in fields:
        w = f.shape[1]
        outs.append(jnp.concatenate([above[:, at:at + w], f, below[:, at:at + w]], axis=0))
        at += w
    return outs


def ring_gather(x, bounds):
    n = lax.axis_size("probe")
    rings = n // 2
    p = lax.axis_index("probe")
    partner = lax.ppermute(x, "probe", [(i, i ^ 1) for i in range(n)])
    pair = jnp.where(p % 2 == 0, jnp.concatenate([x, partner], 1), jnp.concatenate([partner, x], 1))
    ahead = [(i, (i + 2) % n) for i in range(n)]
    behind = [(i, (i - 2) % n) for i in range(n)]
    by_offset = {0: pair}
    fwd = pair
    bwd = pair
    half = rings // 2
    for k in range(1, half):
        fwd = lax.ppermute(fwd, "probe", ahead)
        bwd = lax.ppermute(bwd, "probe", behind)
        by_offset[-k % rings] = fwd
        by_offset[k] = bwd
    cut = x.shape[0] // 2
    far = jnp.concatenate(
        [lax.ppermute(fwd[:cut], "probe", ahead), lax.ppermute(bwd[cut:], "probe", behind)], axis=0
    )
    by_offset[half] = far
    width = pair.shape[1]
    zpos = p // 2
    outs = []
    for lo, hi in bounds:
        buf = jnp.zeros((hi - lo, rings * width, x.shape[2]), x.dtype)
        for d in range(rings):
            at = ((zpos + d) % rings) * width
            buf = lax.dynamic_update_slice_in_dim(buf, by_offset[d][lo:hi], at, 1)
        outs.append(buf)
    return outs


def _ext(win, idx):
    size = win[0].shape[0]
    return win[idx // size][idx % size]


def _depth_terms(win, j, off, rows):
    c = j + HALO

    def at(idx):
        return _ext(win, idx)[off:off + rows]

    whole = _ext(win, c)
    centre = whole[off:off + rows]
    second = (3.0 * SECOND[0]) * centre
    grad = None
    for k in range(1, 5):
        up = at(c + k)
        down = at(c - k)
        second = second + SECOND[k] * (up + down)
        term = FIRST[k] * (up - down)
        grad = term if grad is None else grad + term
    return whole, centre, second, grad


def _slope_kernel(off, lo_ref, hi_ref, mlane_ref, msub_ref, g0_ref, g1_ref, g2_ref):
    n = mlane_ref.shape[0]
    rows = g0_ref.shape[1]
    for j in range(BZ):
        whole, centre, _, grad = _depth_terms((lo_ref, hi_ref), j, off, rows)
        lane = jnp.dot(centre, mlane_ref[...], precision=HI, preferred_element_type=jnp.float32)
        sub = jnp.dot(msub_ref[...], whole, precision=HI, preferred_element_type=jnp.float32)
        g0_ref[j] = grad
        g1_ref[j] = sub[rows:]
        g2_ref[j] = lane[:, n:]


def _image_of(win, j, coef, mlane_ref, msub_ref, off, rows):
    b_ref, g0_ref, g1_ref, g2_ref = coef
    n = mlane_ref.shape[0]
    whole, centre, second, grad = _depth_terms(win, j, off, rows)
    lane = jnp.dot(centre, mlane_ref[...], precision=HI, preferred_element_type=jnp.float32)
    sub = jnp.dot(msub_ref[...], whole, precision=HI, preferred_element_type=jnp.float32)
    second = second + sub[:rows] + lane[:, :n]
    image = (
        b_ref[j] * second
        + g0_ref[j] * grad
        + g1_ref[j] * sub[rows:]
        + g2_ref[j] * lane[:, n:]
    )
    return centre, image


def _op_kernel(flags, *refs):
    with_prev, with_img, want_image, want_step, off = flags
    refs = list(refs)
    lo_ref, hi_ref, b_ref, g0_ref, g1_ref, g2_ref, mlane_ref, msub_ref = refs[:8]
    rest = refs[8:]
    kappa_ref = prev_ref = dk_ref = img_ref = None
    if want_step:
        kappa_ref = rest.pop(0)
        if with_prev:
            prev_ref = rest.pop(0)
        if with_img:
            dk_ref = rest.pop(0)
            img_ref = rest.pop(0)
    outs = rest
    rows = b_ref.shape[1]
    coef = (b_ref, g0_ref, g1_ref, g2_ref)
    for j in range(BZ):
        centre, image = _image_of((lo_ref, hi_ref), j, coef, mlane_ref, msub_ref, off, rows)
        at = 0
        if want_image:
            outs[at][j] = image
            at += 1
        if want_step:
            step = 2.0 * centre + kappa_ref[j] * image
            if with_prev:
                step = step - prev_ref[j]
            if with_img:
                step = step + dk_ref[j] * img_ref[j]
            outs[at][j] = step


def _first_kernel(lo_ref, hi_ref, b_ref, g0_ref, g1_ref, g2_ref, mlane_ref, msub_ref,
                  kappa_ref, prev_ref, part_ref, dk_ref, bg_ref, born_ref):
    rows = b_ref.shape[1]
    coef = (b_ref, g0_ref, g1_ref, g2_ref)
    for j in range(BZ):
        centre, image = _image_of((lo_ref, hi_ref), j, coef, mlane_ref, msub_ref, 0, rows)
        bg_ref[j] = 2.0 * centre - prev_ref[j] + kappa_ref[j] * image
        born_ref[j] = part_ref[j] + dk_ref[j] * image


def _second_kernel(nwin, *refs):
    win1 = refs[:nwin]
    win2 = refs[nwin:2 * nwin]
    b_ref, g0_ref, g1_ref, g2_ref, mlane_ref, msub_ref, kappa_ref, prev_ref, dk_ref = refs[2 * nwin:2 * nwin + 9]
    img_ref, born_ref = refs[-2:]
    rows = b_ref.shape[1]
    coef = (b_ref, g0_ref, g1_ref, g2_ref)
    for j in range(BZ):
        _, image = _image_of(win1, j, coef, mlane_ref, msub_ref, 0, rows)
        img_ref[j] = image
        centre, own = _image_of(win2, j, coef, mlane_ref, msub_ref, 0, rows)
        born_ref[j] = 2.0 * centre - prev_ref[j] + kappa_ref[j] * own + dk_ref[j] * image


def _specs(rows, n, count):
    blk = pl.BlockSpec((BZ, rows, n), lambda i: (i, 0, 0))
    return [blk] * count


def _ext_specs(rows, n):
    return [
        pl.BlockSpec((BZ, rows, n), lambda i: (i, 0, 0)),
        pl.BlockSpec((BZ, rows, n), lambda i: (i + 1, 0, 0)),
    ]


def _mat_specs(mlane, msub):
    return [
        pl.BlockSpec(mlane.shape, lambda i: (0, 0)),
        pl.BlockSpec(msub.shape, lambda i: (0, 0)),
    ]


PARAMS = pltpu.CompilerParams(vmem_limit_bytes=48 * 1024 * 1024)


def slopes_of(b_ext, mlane, msub):
    depth = b_ext.shape[0] - 2 * HALO
    rows_in = b_ext.shape[1]
    rows = msub.shape[0] // 2
    n = b_ext.shape[2]
    shape = jax.ShapeDtypeStruct((depth, rows, n), jnp.float32)
    return pl.pallas_call(
        functools.partial(_slope_kernel, (rows_in - rows) // 2),
        grid=(depth // BZ,),
        in_specs=_ext_specs(rows_in, n) + _mat_specs(mlane, msub),
        out_specs=_specs(rows, n, 3),
        out_shape=[shape] * 3,
        compiler_params=PARAMS,
        interpret=INTERPRET,
    )(b_ext, b_ext, mlane, msub)


def apply_op(f_ext, b, slopes, mlane, msub, kappa=None, prev=None, dk=None, img=None, want_image=False):
    depth = f_ext.shape[0] - 2 * HALO
    rows_in = f_ext.shape[1]
    rows = b.shape[1]
    n = f_ext.shape[2]
    off = (rows_in - rows) // 2
    want_step = kappa is not None
    with_prev = prev is not None
    with_img = img is not None
    args = [f_ext, f_ext, b, *slopes, mlane, msub]
    in_specs = _ext_specs(rows_in, n) + _specs(rows, n, 4) + _mat_specs(mlane, msub)
    if want_step:
        extra = [kappa] + ([prev] if with_prev else []) + ([dk, img] if with_img else [])
        args += extra
        in_specs += _specs(rows, n, len(extra))
    n_out = int(want_image) + int(want_step)
    shape = jax.ShapeDtypeStruct((depth, rows, n), jnp.float32)
    outs = pl.pallas_call(
        functools.partial(_op_kernel, (with_prev, with_img, want_image, want_step, off)),
        grid=(depth // BZ,),
        in_specs=in_specs,
        out_specs=_specs(rows, n, n_out),
        out_shape=[shape] * n_out,
        compiler_params=PARAMS,
        interpret=INTERPRET,
    )(*args)
    return outs


def first_step(u_cur_ext, b, slopes, mlane, msub, kappa, u_prev, partial, dk):
    depth = u_cur_ext.shape[0] - 2 * HALO
    n = u_cur_ext.shape[2]
    shape = jax.ShapeDtypeStruct((depth, n, n), jnp.float32)
    return pl.pallas_call(
        _first_kernel,
        grid=(depth // BZ,),
        in_specs=_ext_specs(n, n) + _specs(n, n, 4) + _mat_specs(mlane, msub) + _specs(n, n, 4),
        out_specs=_specs(n, n, 2),
        out_shape=[shape] * 2,
        compiler_params=PARAMS,
        interpret=INTERPRET,
    )(u_cur_ext, u_cur_ext, b, *slopes, mlane, msub, kappa, u_prev, partial, dk)


def second_inner(bg, born, b, slopes, mlane, msub, kappa, prev, dk):
    depth = bg.shape[0]
    n = bg.shape[2]
    q = HALO
    blocks = depth // BZ
    win = [pl.BlockSpec((q, n, n), lambda i, t=t: ((i + 1) * (BZ // q) - 1 + t, 0, 0)) for t in range(4)]
    inner = [pl.BlockSpec((BZ, n, n), lambda i: (i + 1, 0, 0))]
    shape = jax.ShapeDtypeStruct((depth, n, n), jnp.float32)
    return pl.pallas_call(
        functools.partial(_second_kernel, 4),
        grid=(blocks - 2,),
        in_specs=win * 2 + inner * 4 + _mat_specs(mlane, msub) + inner * 3,
        out_specs=inner * 2,
        out_shape=[shape] * 2,
        compiler_params=PARAMS,
        interpret=INTERPRET,
    )(*([bg] * 4), *([born] * 4), b, *slopes, mlane, msub, kappa, prev, dk)


def _edge_kernel(*refs):
    _second_kernel(2, *refs[:-4], *refs[-2:])


def second_edges(bg_rim, born_rim, b, slopes, mlane, msub, kappa, prev, dk, img, born_out):
    depth = b.shape[0]
    n = b.shape[2]
    last = depth // BZ - 1
    win = [pl.BlockSpec((BZ, n, n), lambda i, t=t: (2 * i + t, 0, 0)) for t in range(2)]
    edge = [pl.BlockSpec((BZ, n, n), lambda i: (i * last, 0, 0))]
    anyspec = [pl.BlockSpec(memory_space=pl.ANY)]
    shape = jax.ShapeDtypeStruct((depth, n, n), jnp.float32)
    return pl.pallas_call(
        _edge_kernel,
        grid=(2,),
        in_specs=win * 2 + edge * 4 + _mat_specs(mlane, msub) + edge * 3 + anyspec * 2,
        out_specs=edge * 2,
        out_shape=[shape] * 2,
        input_output_aliases={13: 0, 14: 1},
        compiler_params=PARAMS,
        interpret=INTERPRET,
    )(bg_rim, bg_rim, born_rim, born_rim, b, *slopes, mlane, msub, kappa, prev, dk, img, born_out)


def depth_rims(fields):
    count = lax.axis_size("slab")
    ends = count - 1
    heads = jnp.concatenate([f[:HALO] for f in fields], axis=1)
    tails = jnp.concatenate([f[f.shape[0] - HALO:] for f in fields], axis=1)
    above = lax.ppermute(tails, "slab", [(i, i + 1) for i in range(ends)])
    below = lax.ppermute(heads, "slab", [(i + 1, i) for i in range(ends)])
    outs = []
    at = 0
    span = BZ + HALO
    for f in fields:
        w = f.shape[1]
        d = f.shape[0]
        outs.append(jnp.concatenate(
            [above[:, at:at + w], f[:span], f[d - span:], below[:, at:at + w]], axis=0))
        at += w
    return outs


def local_body(u_prev, u_cur, buoyancy, kappa, dkappa, du_prev, du_cur):
    n = buoyancy.shape[1]
    strip = u_cur.shape[1]
    offset = lax.axis_index("probe") * strip
    ms, mg = band_matrices(n)
    mlane = jnp.asarray(np.concatenate([ms, mg.T], axis=1))
    msub = jnp.asarray(np.concatenate([ms, mg], axis=0))

    depth = u_cur.shape[0]
    cur_rows = depth + 2 * HALO
    probe_kappa = dkappa[0]
    older = du_prev[0]
    newer = du_cur[0]
    u_cur_strip_ext, buoyancy_ext, newer_ext = halo_depth_many([u_cur, buoyancy, newer])
    u_cur_ext, u_prev_all = ring_gather(
        jnp.concatenate([u_cur_strip_ext, u_prev], axis=0),
        ((0, cur_rows), (cur_rows, cur_rows + depth)),
    )

    slopes = slopes_of(buoyancy_ext, mlane, msub)

    (partial_first,) = apply_op(newer_ext, buoyancy, slopes, mlane, msub, kappa=kappa, prev=older)

    background_first, born_first = first_step(
        u_cur_ext, buoyancy, slopes, mlane, msub, kappa, u_prev_all, partial_first, probe_kappa
    )

    bg_rim, born_rim = depth_rims([background_first, born_first])
    image_second, born_second = second_inner(
        background_first, born_first, buoyancy, slopes, mlane, msub, kappa, newer, probe_kappa
    )
    image_second, born_second = second_edges(
        bg_rim, born_rim, buoyancy, slopes, mlane, msub, kappa, newer, probe_kappa,
        image_second, born_second,
    )

    def cut_strip(field):
        return lax.dynamic_slice_in_dim(field, offset, strip, 1)

    background_first_strip = cut_strip(background_first)
    background_second = (
        2.0 * background_first_strip - u_cur + cut_strip(kappa) * cut_strip(image_second)
    )
    return background_first_strip, background_second, born_first[None], born_second[None]


def solution(mesh):
    return shard_mapped(mesh)


def shard_mapped(mesh):
    return jax.shard_map(
        local_body,
        mesh=mesh,
        in_specs=(
            P("slab", "probe", None),
            P("slab", "probe", None),
            P("slab", None, None),
            P("slab", None, None),
            P("probe", "slab", None, None),
            P("probe", "slab", None, None),
            P("probe", "slab", None, None),
        ),
        out_specs=(
            P("slab", "probe", None),
            P("slab", "probe", None),
            P("probe", "slab", None, None),
            P("probe", "slab", None, None),
        ),
        check_vma=False,
    )
```

```python
import functools

import numpy as np
import jax
import jax.numpy as jnp
from jax import lax
from jax.experimental import pallas as pl
from jax.experimental.pallas import tpu as pltpu
from jax.sharding import PartitionSpec as P


SECOND = (-205.0 / 72.0, 8.0 / 5.0, -1.0 / 5.0, 8.0 / 315.0, -1.0 / 560.0)
FIRST = (0.0, 4.0 / 5.0, -1.0 / 5.0, 4.0 / 105.0, -1.0 / 280.0)

BZ = 8
HALO = 4
INTERPRET = False
HI = lax.Precision.HIGHEST


def band_matrices(n):
    ms = np.zeros((n, n), np.float32)
    mg = np.zeros((n, n), np.float32)
    for i in range(n):
        for k in range(1, 5):
            for j, sign in ((i + k, 1.0), (i - k, -1.0)):
                if 0 <= j < n:
                    ms[i, j] = SECOND[k]
                    mg[i, j] = sign * FIRST[k]
    return ms, mg


def halo_depth_many(fields):
    count = lax.axis_size("slab")
    ends = count - 1
    heads = jnp.concatenate([f[:HALO] for f in fields], axis=1)
    tails = jnp.concatenate([f[f.shape[0] - HALO:] for f in fields], axis=1)
    above = lax.ppermute(tails, "slab", [(i, i + 1) for i in range(ends)])
    below = lax.ppermute(heads, "slab", [(i + 1, i) for i in range(ends)])
    outs = []
    at = 0
    for f in fields:
        w = f.shape[1]
        outs.append(jnp.concatenate([above[:, at:at + w], f, below[:, at:at + w]], axis=0))
        at += w
    return outs


def ring_gather(x, bounds):
    n = lax.axis_size("probe")
    rings = n // 2
    p = lax.axis_index("probe")
    partner = lax.ppermute(x, "probe", [(i, i ^ 1) for i in range(n)])
    pair = jnp.where(p % 2 == 0, jnp.concatenate([x, partner], 1), jnp.concatenate([partner, x], 1))
    ahead = [(i, (i + 2) % n) for i in range(n)]
    behind = [(i, (i - 2) % n) for i in range(n)]
    by_offset = {0: pair}
    fwd = pair
    bwd = pair
    half = rings // 2
    for k in range(1, half):
        fwd = lax.ppermute(fwd, "probe", ahead)
        bwd = lax.ppermute(bwd, "probe", behind)
        by_offset[-k % rings] = fwd
        by_offset[k] = bwd
    cut = x.shape[0] // 2
    far = jnp.concatenate(
        [lax.ppermute(fwd[:cut], "probe", ahead), lax.ppermute(bwd[cut:], "probe", behind)], axis=0
    )
    by_offset[half] = far
    width = pair.shape[1]
    zpos = p // 2
    outs = []
    for lo, hi in bounds:
        buf = jnp.zeros((hi - lo, rings * width, x.shape[2]), x.dtype)
        for d in range(rings):
            at = ((zpos + d) % rings) * width
            buf = lax.dynamic_update_slice_in_dim(buf, by_offset[d][lo:hi], at, 1)
        outs.append(buf)
    return outs


def _ext(win, idx):
    size = win[0].shape[0]
    return win[idx // size][idx % size]


def _depth_terms(win, j, off, rows):
    c = j + HALO

    def at(idx):
        return _ext(win, idx)[off:off + rows]

    whole = _ext(win, c)
    centre = whole[off:off + rows]
    second = (3.0 * SECOND[0]) * centre
    grad = None
    for k in range(1, 5):
        up = at(c + k)
        down = at(c - k)
        second = second + SECOND[k] * (up + down)
        term = FIRST[k] * (up - down)
        grad = term if grad is None else grad + term
    return whole, centre, second, grad


def _slope_kernel(off, lo_ref, hi_ref, mlane_ref, msub_ref, g0_ref, g1_ref, g2_ref):
    n = mlane_ref.shape[0]
    rows = g0_ref.shape[1]
    for j in range(BZ):
        whole, centre, _, grad = _depth_terms((lo_ref, hi_ref), j, off, rows)
        lane = jnp.dot(centre, mlane_ref[...], precision=HI, preferred_element_type=jnp.float32)
        sub = jnp.dot(msub_ref[...], whole, precision=HI, preferred_element_type=jnp.float32)
        g0_ref[j] = grad
        g1_ref[j] = sub[rows:]
        g2_ref[j] = lane[:, n:]


def _image_of(win, j, coef, mlane_ref, msub_ref, off, rows):
    b_ref, g0_ref, g1_ref, g2_ref = coef
    n = mlane_ref.shape[0]
    whole, centre, second, grad = _depth_terms(win, j, off, rows)
    lane = jnp.dot(centre, mlane_ref[...], precision=HI, preferred_element_type=jnp.float32)
    sub = jnp.dot(msub_ref[...], whole, precision=HI, preferred_element_type=jnp.float32)
    second = second + sub[:rows] + lane[:, :n]
    image = (
        b_ref[j] * second
        + g0_ref[j] * grad
        + g1_ref[j] * sub[rows:]
        + g2_ref[j] * lane[:, n:]
    )
    return centre, image


def _op_kernel(flags, *refs):
    with_prev, with_img, want_image, want_step, off = flags
    refs = list(refs)
    lo_ref, hi_ref, b_ref, g0_ref, g1_ref, g2_ref, mlane_ref, msub_ref = refs[:8]
    rest = refs[8:]
    kappa_ref = prev_ref = dk_ref = img_ref = None
    if want_step:
        kappa_ref = rest.pop(0)
        if with_prev:
            prev_ref = rest.pop(0)
        if with_img:
            dk_ref = rest.pop(0)
            img_ref = rest.pop(0)
    outs = rest
    rows = b_ref.shape[1]
    coef = (b_ref, g0_ref, g1_ref, g2_ref)
    for j in range(BZ):
        centre, image = _image_of((lo_ref, hi_ref), j, coef, mlane_ref, msub_ref, off, rows)
        at = 0
        if want_image:
            outs[at][j] = image
            at += 1
        if want_step:
            step = 2.0 * centre + kappa_ref[j] * image
            if with_prev:
                step = step - prev_ref[j]
            if with_img:
                step = step + dk_ref[j] * img_ref[j]
            outs[at][j] = step


def _first_kernel(lo_ref, hi_ref, b_ref, g0_ref, g1_ref, g2_ref, mlane_ref, msub_ref,
                  kappa_ref, prev_ref, part_ref, dk_ref, bg_ref, born_ref):
    rows = b_ref.shape[1]
    coef = (b_ref, g0_ref, g1_ref, g2_ref)
    for j in range(BZ):
        centre, image = _image_of((lo_ref, hi_ref), j, coef, mlane_ref, msub_ref, 0, rows)
        bg_ref[j] = 2.0 * centre - prev_ref[j] + kappa_ref[j] * image
        born_ref[j] = part_ref[j] + dk_ref[j] * image


def _second_kernel(nwin, *refs):
    win1 = refs[:nwin]
    win2 = refs[nwin:2 * nwin]
    b_ref, g0_ref, g1_ref, g2_ref, mlane_ref, msub_ref, kappa_ref, prev_ref, dk_ref = refs[2 * nwin:2 * nwin + 9]
    img_ref, born_ref = refs[-2:]
    rows = b_ref.shape[1]
    coef = (b_ref, g0_ref, g1_ref, g2_ref)
    for j in range(b_ref.shape[0]):
        _, image = _image_of(win1, j, coef, mlane_ref, msub_ref, 0, rows)
        img_ref[j] = image
        centre, own = _image_of(win2, j, coef, mlane_ref, msub_ref, 0, rows)
        born_ref[j] = 2.0 * centre - prev_ref[j] + kappa_ref[j] * own + dk_ref[j] * image


def _specs(rows, n, count):
    blk = pl.BlockSpec((BZ, rows, n), lambda i: (i, 0, 0))
    return [blk] * count


def _ext_specs(rows, n):
    return [
        pl.BlockSpec((BZ, rows, n), lambda i: (i, 0, 0)),
        pl.BlockSpec((BZ, rows, n), lambda i: (i + 1, 0, 0)),
    ]


def _mat_specs(mlane, msub):
    return [
        pl.BlockSpec(mlane.shape, lambda i: (0, 0)),
        pl.BlockSpec(msub.shape, lambda i: (0, 0)),
    ]


PARAMS = pltpu.CompilerParams(vmem_limit_bytes=48 * 1024 * 1024)


def slopes_of(b_ext, mlane, msub):
    depth = b_ext.shape[0] - 2 * HALO
    rows_in = b_ext.shape[1]
    rows = msub.shape[0] // 2
    n = b_ext.shape[2]
    shape = jax.ShapeDtypeStruct((depth, rows, n), jnp.float32)
    return pl.pallas_call(
        functools.partial(_slope_kernel, (rows_in - rows) // 2),
        grid=(depth // BZ,),
        in_specs=_ext_specs(rows_in, n) + _mat_specs(mlane, msub),
        out_specs=_specs(rows, n, 3),
        out_shape=[shape] * 3,
        compiler_params=PARAMS,
        interpret=INTERPRET,
    )(b_ext, b_ext, mlane, msub)


def apply_op(f_ext, b, slopes, mlane, msub, kappa=None, prev=None, dk=None, img=None, want_image=False):
    depth = f_ext.shape[0] - 2 * HALO
    rows_in = f_ext.shape[1]
    rows = b.shape[1]
    n = f_ext.shape[2]
    off = (rows_in - rows) // 2
    want_step = kappa is not None
    with_prev = prev is not None
    with_img = img is not None
    args = [f_ext, f_ext, b, *slopes, mlane, msub]
    in_specs = _ext_specs(rows_in, n) + _specs(rows, n, 4) + _mat_specs(mlane, msub)
    if want_step:
        extra = [kappa] + ([prev] if with_prev else []) + ([dk, img] if with_img else [])
        args += extra
        in_specs += _specs(rows, n, len(extra))
    n_out = int(want_image) + int(want_step)
    shape = jax.ShapeDtypeStruct((depth, rows, n), jnp.float32)
    outs = pl.pallas_call(
        functools.partial(_op_kernel, (with_prev, with_img, want_image, want_step, off)),
        grid=(depth // BZ,),
        in_specs=in_specs,
        out_specs=_specs(rows, n, n_out),
        out_shape=[shape] * n_out,
        compiler_params=PARAMS,
        interpret=INTERPRET,
    )(*args)
    return outs


def first_step(u_cur_ext, b, slopes, mlane, msub, kappa, u_prev, partial, dk):
    depth = u_cur_ext.shape[0] - 2 * HALO
    n = u_cur_ext.shape[2]
    shape = jax.ShapeDtypeStruct((depth, n, n), jnp.float32)
    return pl.pallas_call(
        _first_kernel,
        grid=(depth // BZ,),
        in_specs=_ext_specs(n, n) + _specs(n, n, 4) + _mat_specs(mlane, msub) + _specs(n, n, 4),
        out_specs=_specs(n, n, 2),
        out_shape=[shape] * 2,
        compiler_params=PARAMS,
        interpret=INTERPRET,
    )(u_cur_ext, u_cur_ext, b, *slopes, mlane, msub, kappa, u_prev, partial, dk)


QB = HALO


def second_inner(bg, born, b, slopes, mlane, msub, kappa, prev, dk):
    depth = bg.shape[0]
    n = bg.shape[2]
    blocks = depth // QB
    win = [pl.BlockSpec((QB, n, n), lambda i, t=t: (i + t, 0, 0)) for t in range(3)]
    inner = [pl.BlockSpec((QB, n, n), lambda i: (i + 1, 0, 0))]
    shape = jax.ShapeDtypeStruct((depth, n, n), jnp.float32)
    return pl.pallas_call(
        functools.partial(_second_kernel, 3),
        grid=(blocks - 2,),
        in_specs=win * 2 + inner * 4 + _mat_specs(mlane, msub) + inner * 3,
        out_specs=inner * 2,
        out_shape=[shape] * 2,
        compiler_params=PARAMS,
        interpret=INTERPRET,
    )(*([bg] * 3), *([born] * 3), b, *slopes, mlane, msub, kappa, prev, dk)


def _edge_kernel(*refs):
    _second_kernel(3, *refs[:-4], *refs[-2:])


def second_edges(bg_rim, born_rim, b, slopes, mlane, msub, kappa, prev, dk, img, born_out):
    depth = b.shape[0]
    n = b.shape[2]
    last = depth // QB - 1
    win = [pl.BlockSpec((QB, n, n), lambda i, t=t: (3 * i + t, 0, 0)) for t in range(3)]
    edge = [pl.BlockSpec((QB, n, n), lambda i: (i * last, 0, 0))]
    anyspec = [pl.BlockSpec(memory_space=pl.ANY)]
    shape = jax.ShapeDtypeStruct((depth, n, n), jnp.float32)
    return pl.pallas_call(
        _edge_kernel,
        grid=(2,),
        in_specs=win * 2 + edge * 4 + _mat_specs(mlane, msub) + edge * 3 + anyspec * 2,
        out_specs=edge * 2,
        out_shape=[shape] * 2,
        input_output_aliases={15: 0, 16: 1},
        compiler_params=PARAMS,
        interpret=INTERPRET,
    )(*([bg_rim] * 3), *([born_rim] * 3), b, *slopes, mlane, msub, kappa, prev, dk, img, born_out)


def depth_rims(fields):
    count = lax.axis_size("slab")
    ends = count - 1
    heads = jnp.concatenate([f[:HALO] for f in fields], axis=1)
    tails = jnp.concatenate([f[f.shape[0] - HALO:] for f in fields], axis=1)
    above = lax.ppermute(tails, "slab", [(i, i + 1) for i in range(ends)])
    below = lax.ppermute(heads, "slab", [(i + 1, i) for i in range(ends)])
    outs = []
    at = 0
    span = QB + HALO
    for f in fields:
        w = f.shape[1]
        d = f.shape[0]
        outs.append(jnp.concatenate(
            [above[:, at:at + w], f[:span], f[d - span:], below[:, at:at + w]], axis=0))
        at += w
    return outs


def local_body(u_prev, u_cur, buoyancy, kappa, dkappa, du_prev, du_cur):
    n = buoyancy.shape[1]
    strip = u_cur.shape[1]
    offset = lax.axis_index("probe") * strip
    ms, mg = band_matrices(n)
    mlane = jnp.asarray(np.concatenate([ms, mg.T], axis=1))
    msub = jnp.asarray(np.concatenate([ms, mg], axis=0))

    depth = u_cur.shape[0]
    probe_kappa = dkappa[0]
    older = du_prev[0]
    newer = du_cur[0]
    u_cur_strip_ext, buoyancy_ext, newer_ext = halo_depth_many([u_cur, buoyancy, newer])
    rims = jnp.concatenate([u_cur_strip_ext[:HALO], u_cur_strip_ext[depth + HALO:]], axis=0)
    rims_all = lax.all_gather(rims, "probe", axis=1, tiled=True)
    u_cur_all, u_prev_all = ring_gather(
        jnp.concatenate([u_cur, u_prev], axis=0), ((0, depth), (depth, 2 * depth))
    )
    u_cur_ext = jnp.concatenate([rims_all[:HALO], u_cur_all, rims_all[HALO:]], axis=0)

    slopes = slopes_of(buoyancy_ext, mlane, msub)

    (partial_first,) = apply_op(newer_ext, buoyancy, slopes, mlane, msub, kappa=kappa, prev=older)

    background_first, born_first = first_step(
        u_cur_ext, buoyancy, slopes, mlane, msub, kappa, u_prev_all, partial_first, probe_kappa
    )

    bg_rim, born_rim = depth_rims([background_first, born_first])
    image_second, born_second = second_inner(
        background_first, born_first, buoyancy, slopes, mlane, msub, kappa, newer, probe_kappa
    )
    image_second, born_second = second_edges(
        bg_rim, born_rim, buoyancy, slopes, mlane, msub, kappa, newer, probe_kappa,
        image_second, born_second,
    )

    def cut_strip(field):
        return lax.dynamic_slice_in_dim(field, offset, strip, 1)

    background_first_strip = cut_strip(background_first)
    background_second = (
        2.0 * background_first_strip - u_cur + cut_strip(kappa) * cut_strip(image_second)
    )
    return background_first_strip, background_second, born_first[None], born_second[None]


def solution(mesh):
    return shard_mapped(mesh)


def shard_mapped(mesh):
    return jax.shard_map(
        local_body,
        mesh=mesh,
        in_specs=(
            P("slab", "probe", None),
            P("slab", "probe", None),
            P("slab", None, None),
            P("slab", None, None),
            P("probe", "slab", None, None),
            P("probe", "slab", None, None),
            P("probe", "slab", None, None),
        ),
        out_specs=(
            P("slab", "probe", None),
            P("slab", "probe", None),
            P("probe", "slab", None, None),
            P("probe", "slab", None, None),
        ),
        check_vma=False,
    )
```

```python
import functools

import numpy as np
import jax
import jax.numpy as jnp
from jax import lax
from jax.experimental import pallas as pl
from jax.experimental.pallas import tpu as pltpu
from jax.sharding import PartitionSpec as P


SECOND = (-205.0 / 72.0, 8.0 / 5.0, -1.0 / 5.0, 8.0 / 315.0, -1.0 / 560.0)
FIRST = (0.0, 4.0 / 5.0, -1.0 / 5.0, 4.0 / 105.0, -1.0 / 280.0)

BZ = 8
HALO = 4
INTERPRET = False
HI = lax.Precision.HIGHEST


def band_matrices(n):
    ms = np.zeros((n, n), np.float32)
    mg = np.zeros((n, n), np.float32)
    for i in range(n):
        for k in range(1, 5):
            for j, sign in ((i + k, 1.0), (i - k, -1.0)):
                if 0 <= j < n:
                    ms[i, j] = SECOND[k]
                    mg[i, j] = sign * FIRST[k]
    return ms, mg


def halo_depth_many(fields):
    count = lax.axis_size("slab")
    ends = count - 1
    heads = jnp.concatenate([f[:HALO] for f in fields], axis=1)
    tails = jnp.concatenate([f[f.shape[0] - HALO:] for f in fields], axis=1)
    above = lax.ppermute(tails, "slab", [(i, i + 1) for i in range(ends)])
    below = lax.ppermute(heads, "slab", [(i + 1, i) for i in range(ends)])
    outs = []
    at = 0
    for f in fields:
        w = f.shape[1]
        outs.append(jnp.concatenate([above[:, at:at + w], f, below[:, at:at + w]], axis=0))
        at += w
    return outs


def ring_gather(x, bounds):
    n = lax.axis_size("probe")
    rings = n // 2
    p = lax.axis_index("probe")
    partner = lax.ppermute(x, "probe", [(i, i ^ 1) for i in range(n)])
    pair = jnp.where(p % 2 == 0, jnp.concatenate([x, partner], 1), jnp.concatenate([partner, x], 1))
    ahead = [(i, (i + 2) % n) for i in range(n)]
    behind = [(i, (i - 2) % n) for i in range(n)]
    by_offset = {0: pair}
    fwd = pair
    bwd = pair
    half = rings // 2
    for k in range(1, half):
        fwd = lax.ppermute(fwd, "probe", ahead)
        bwd = lax.ppermute(bwd, "probe", behind)
        by_offset[-k % rings] = fwd
        by_offset[k] = bwd
    cut = x.shape[0] // 2
    far = jnp.concatenate(
        [lax.ppermute(fwd[:cut], "probe", ahead), lax.ppermute(bwd[cut:], "probe", behind)], axis=0
    )
    by_offset[half] = far
    width = pair.shape[1]
    zpos = p // 2
    outs = []
    for lo, hi in bounds:
        buf = jnp.zeros((hi - lo, rings * width, x.shape[2]), x.dtype)
        for d in range(rings):
            at = ((zpos + d) % rings) * width
            buf = lax.dynamic_update_slice_in_dim(buf, by_offset[d][lo:hi], at, 1)
        outs.append(buf)
    return outs


def _ext(win, idx):
    size = win[0].shape[0]
    return win[idx // size][idx % size]


def _depth_terms(win, j, off, rows):
    c = j + HALO

    def at(idx):
        return _ext(win, idx)[off:off + rows]

    whole = _ext(win, c)
    centre = whole[off:off + rows]
    second = (3.0 * SECOND[0]) * centre
    grad = None
    for k in range(1, 5):
        up = at(c + k)
        down = at(c - k)
        second = second + SECOND[k] * (up + down)
        term = FIRST[k] * (up - down)
        grad = term if grad is None else grad + term
    return whole, centre, second, grad


def _slope_kernel(off, lo_ref, hi_ref, mlane_ref, msub_ref, g0_ref, g1_ref, g2_ref):
    n = mlane_ref.shape[0]
    rows = g0_ref.shape[1]
    for j in range(BZ):
        whole, centre, _, grad = _depth_terms((lo_ref, hi_ref), j, off, rows)
        lane = jnp.dot(centre, mlane_ref[...], precision=HI, preferred_element_type=jnp.float32)
        sub = jnp.dot(msub_ref[...], whole, precision=HI, preferred_element_type=jnp.float32)
        g0_ref[j] = grad
        g1_ref[j] = sub[rows:]
        g2_ref[j] = lane[:, n:]


def _image_of(win, j, coef, mlane_ref, msub_ref, off, rows):
    b_ref, g0_ref, g1_ref, g2_ref = coef
    n = mlane_ref.shape[0]
    whole, centre, second, grad = _depth_terms(win, j, off, rows)
    lane = jnp.dot(centre, mlane_ref[...], precision=HI, preferred_element_type=jnp.float32)
    sub = jnp.dot(msub_ref[...], whole, precision=HI, preferred_element_type=jnp.float32)
    second = second + sub[:rows] + lane[:, :n]
    image = (
        b_ref[j] * second
        + g0_ref[j] * grad
        + g1_ref[j] * sub[rows:]
        + g2_ref[j] * lane[:, n:]
    )
    return centre, image


def _op_kernel(flags, *refs):
    with_prev, with_img, want_image, want_step, off = flags
    refs = list(refs)
    lo_ref, hi_ref, b_ref, g0_ref, g1_ref, g2_ref, mlane_ref, msub_ref = refs[:8]
    rest = refs[8:]
    kappa_ref = prev_ref = dk_ref = img_ref = None
    if want_step:
        kappa_ref = rest.pop(0)
        if with_prev:
            prev_ref = rest.pop(0)
        if with_img:
            dk_ref = rest.pop(0)
            img_ref = rest.pop(0)
    outs = rest
    rows = b_ref.shape[1]
    coef = (b_ref, g0_ref, g1_ref, g2_ref)
    for j in range(BZ):
        centre, image = _image_of((lo_ref, hi_ref), j, coef, mlane_ref, msub_ref, off, rows)
        at = 0
        if want_image:
            outs[at][j] = image
            at += 1
        if want_step:
            step = 2.0 * centre + kappa_ref[j] * image
            if with_prev:
                step = step - prev_ref[j]
            if with_img:
                step = step + dk_ref[j] * img_ref[j]
            outs[at][j] = step


def _first_kernel(lo_ref, hi_ref, b_ref, g0_ref, g1_ref, g2_ref, mlane_ref, msub_ref,
                  kappa_ref, prev_ref, part_ref, dk_ref, bg_ref, born_ref):
    rows = b_ref.shape[1]
    coef = (b_ref, g0_ref, g1_ref, g2_ref)
    for j in range(BZ):
        centre, image = _image_of((lo_ref, hi_ref), j, coef, mlane_ref, msub_ref, 0, rows)
        bg_ref[j] = 2.0 * centre - prev_ref[j] + kappa_ref[j] * image
        born_ref[j] = part_ref[j] + dk_ref[j] * image


def _second_kernel(nwin, *refs):
    win1 = refs[:nwin]
    win2 = refs[nwin:2 * nwin]
    b_ref, g0_ref, g1_ref, g2_ref, mlane_ref, msub_ref, kappa_ref, prev_ref, dk_ref = refs[2 * nwin:2 * nwin + 9]
    img_ref, born_ref = refs[-2:]
    rows = b_ref.shape[1]
    coef = (b_ref, g0_ref, g1_ref, g2_ref)
    for j in range(b_ref.shape[0]):
        _, image = _image_of(win1, j, coef, mlane_ref, msub_ref, 0, rows)
        img_ref[j] = image
        centre, own = _image_of(win2, j, coef, mlane_ref, msub_ref, 0, rows)
        born_ref[j] = 2.0 * centre - prev_ref[j] + kappa_ref[j] * own + dk_ref[j] * image


def _specs(rows, n, count):
    blk = pl.BlockSpec((BZ, rows, n), lambda i: (i, 0, 0))
    return [blk] * count


def _ext_specs(rows, n):
    return [
        pl.BlockSpec((BZ, rows, n), lambda i: (i, 0, 0)),
        pl.BlockSpec((BZ, rows, n), lambda i: (i + 1, 0, 0)),
    ]


def _mat_specs(mlane, msub):
    return [
        pl.BlockSpec(mlane.shape, lambda i: (0, 0)),
        pl.BlockSpec(msub.shape, lambda i: (0, 0)),
    ]


PARAMS = pltpu.CompilerParams(vmem_limit_bytes=48 * 1024 * 1024)


def slopes_of(b_ext, mlane, msub):
    depth = b_ext.shape[0] - 2 * HALO
    rows_in = b_ext.shape[1]
    rows = msub.shape[0] // 2
    n = b_ext.shape[2]
    shape = jax.ShapeDtypeStruct((depth, rows, n), jnp.float32)
    return pl.pallas_call(
        functools.partial(_slope_kernel, (rows_in - rows) // 2),
        grid=(depth // BZ,),
        in_specs=_ext_specs(rows_in, n) + _mat_specs(mlane, msub),
        out_specs=_specs(rows, n, 3),
        out_shape=[shape] * 3,
        compiler_params=PARAMS,
        interpret=INTERPRET,
    )(b_ext, b_ext, mlane, msub)


def apply_op(f_ext, b, slopes, mlane, msub, kappa=None, prev=None, dk=None, img=None, want_image=False):
    depth = f_ext.shape[0] - 2 * HALO
    rows_in = f_ext.shape[1]
    rows = b.shape[1]
    n = f_ext.shape[2]
    off = (rows_in - rows) // 2
    want_step = kappa is not None
    with_prev = prev is not None
    with_img = img is not None
    args = [f_ext, f_ext, b, *slopes, mlane, msub]
    in_specs = _ext_specs(rows_in, n) + _specs(rows, n, 4) + _mat_specs(mlane, msub)
    if want_step:
        extra = [kappa] + ([prev] if with_prev else []) + ([dk, img] if with_img else [])
        args += extra
        in_specs += _specs(rows, n, len(extra))
    n_out = int(want_image) + int(want_step)
    shape = jax.ShapeDtypeStruct((depth, rows, n), jnp.float32)
    outs = pl.pallas_call(
        functools.partial(_op_kernel, (with_prev, with_img, want_image, want_step, off)),
        grid=(depth // BZ,),
        in_specs=in_specs,
        out_specs=_specs(rows, n, n_out),
        out_shape=[shape] * n_out,
        compiler_params=PARAMS,
        interpret=INTERPRET,
    )(*args)
    return outs


def first_step(u_cur_ext, b, slopes, mlane, msub, kappa, u_prev, partial, dk):
    depth = u_cur_ext.shape[0] - 2 * HALO
    n = u_cur_ext.shape[2]
    shape = jax.ShapeDtypeStruct((depth, n, n), jnp.float32)
    return pl.pallas_call(
        _first_kernel,
        grid=(depth // BZ,),
        in_specs=_ext_specs(n, n) + _specs(n, n, 4) + _mat_specs(mlane, msub) + _specs(n, n, 4),
        out_specs=_specs(n, n, 2),
        out_shape=[shape] * 2,
        compiler_params=PARAMS,
        interpret=INTERPRET,
    )(u_cur_ext, u_cur_ext, b, *slopes, mlane, msub, kappa, u_prev, partial, dk)


QB = HALO


def second_inner(bg, born, b, slopes, mlane, msub, kappa, prev, dk):
    depth = bg.shape[0]
    n = bg.shape[2]
    blocks = depth // QB
    win = [pl.BlockSpec((QB, n, n), lambda i, t=t: (i + t, 0, 0)) for t in range(3)]
    inner = [pl.BlockSpec((QB, n, n), lambda i: (i + 1, 0, 0))]
    shape = jax.ShapeDtypeStruct((depth, n, n), jnp.float32)
    return pl.pallas_call(
        functools.partial(_second_kernel, 3),
        grid=(blocks - 2,),
        in_specs=win * 2 + inner * 4 + _mat_specs(mlane, msub) + inner * 3,
        out_specs=inner * 2,
        out_shape=[shape] * 2,
        compiler_params=PARAMS,
        interpret=INTERPRET,
    )(*([bg] * 3), *([born] * 3), b, *slopes, mlane, msub, kappa, prev, dk)


def _edge_kernel(*refs):
    _second_kernel(3, *refs[:-4], *refs[-2:])


def second_edges(bg_rim, born_rim, b, slopes, mlane, msub, kappa, prev, dk, img, born_out):
    depth = b.shape[0]
    n = b.shape[2]
    last = depth // QB - 1
    win = [pl.BlockSpec((QB, n, n), lambda i, t=t: (3 * i + t, 0, 0)) for t in range(3)]
    edge = [pl.BlockSpec((QB, n, n), lambda i: (i * last, 0, 0))]
    anyspec = [pl.BlockSpec(memory_space=pl.ANY)]
    shape = jax.ShapeDtypeStruct((depth, n, n), jnp.float32)
    return pl.pallas_call(
        _edge_kernel,
        grid=(2,),
        in_specs=win * 2 + edge * 4 + _mat_specs(mlane, msub) + edge * 3 + anyspec * 2,
        out_specs=edge * 2,
        out_shape=[shape] * 2,
        input_output_aliases={15: 0, 16: 1},
        compiler_params=PARAMS,
        interpret=INTERPRET,
    )(*([bg_rim] * 3), *([born_rim] * 3), b, *slopes, mlane, msub, kappa, prev, dk, img, born_out)


def depth_rims(fields):
    count = lax.axis_size("slab")
    ends = count - 1
    heads = jnp.concatenate([f[:HALO] for f in fields], axis=1)
    tails = jnp.concatenate([f[f.shape[0] - HALO:] for f in fields], axis=1)
    above = lax.ppermute(tails, "slab", [(i, i + 1) for i in range(ends)])
    below = lax.ppermute(heads, "slab", [(i + 1, i) for i in range(ends)])
    outs = []
    at = 0
    span = QB + HALO
    for f in fields:
        w = f.shape[1]
        d = f.shape[0]
        outs.append(jnp.concatenate(
            [above[:, at:at + w], f[:span], f[d - span:], below[:, at:at + w]], axis=0))
        at += w
    return outs


def local_body(u_prev, u_cur, buoyancy, kappa, dkappa, du_prev, du_cur):
    n = buoyancy.shape[1]
    strip = u_cur.shape[1]
    offset = lax.axis_index("probe") * strip
    ms, mg = band_matrices(n)
    mlane = jnp.asarray(np.concatenate([ms, mg.T], axis=1))
    msub = jnp.asarray(np.concatenate([ms, mg], axis=0))

    depth = u_cur.shape[0]
    cur_rows = depth + 2 * HALO
    probe_kappa = dkappa[0]
    older = du_prev[0]
    newer = du_cur[0]
    (u_cur_strip_ext,) = halo_depth_many([u_cur])
    buoyancy_ext, newer_ext = halo_depth_many([buoyancy, newer])
    u_cur_ext, u_prev_all = ring_gather(
        jnp.concatenate([u_cur_strip_ext, u_prev], axis=0),
        ((0, cur_rows), (cur_rows, cur_rows + depth)),
    )

    slopes = slopes_of(buoyancy_ext, mlane, msub)

    (partial_first,) = apply_op(newer_ext, buoyancy, slopes, mlane, msub, kappa=kappa, prev=older)

    background_first, born_first = first_step(
        u_cur_ext, buoyancy, slopes, mlane, msub, kappa, u_prev_all, partial_first, probe_kappa
    )

    bg_rim, born_rim = depth_rims([background_first, born_first])
    image_second, born_second = second_inner(
        background_first, born_first, buoyancy, slopes, mlane, msub, kappa, newer, probe_kappa
    )
    image_second, born_second = second_edges(
        bg_rim, born_rim, buoyancy, slopes, mlane, msub, kappa, newer, probe_kappa,
        image_second, born_second,
    )

    def cut_strip(field):
        return lax.dynamic_slice_in_dim(field, offset, strip, 1)

    background_first_strip = cut_strip(background_first)
    background_second = (
        2.0 * background_first_strip - u_cur + cut_strip(kappa) * cut_strip(image_second)
    )
    return background_first_strip, background_second, born_first[None], born_second[None]


def solution(mesh):
    return shard_mapped(mesh)


def shard_mapped(mesh):
    return jax.shard_map(
        local_body,
        mesh=mesh,
        in_specs=(
            P("slab", "probe", None),
            P("slab", "probe", None),
            P("slab", None, None),
            P("slab", None, None),
            P("probe", "slab", None, None),
            P("probe", "slab", None, None),
            P("probe", "slab", None, None),
        ),
        out_specs=(
            P("slab", "probe", None),
            P("slab", "probe", None),
            P("probe", "slab", None, None),
            P("probe", "slab", None, None),
        ),
        check_vma=False,
    )
```

```python
import functools

import numpy as np
import jax
import jax.numpy as jnp
from jax import lax
from jax.experimental import pallas as pl
from jax.experimental.pallas import tpu as pltpu
from jax.sharding import PartitionSpec as P


SECOND = (-205.0 / 72.0, 8.0 / 5.0, -1.0 / 5.0, 8.0 / 315.0, -1.0 / 560.0)
FIRST = (0.0, 4.0 / 5.0, -1.0 / 5.0, 4.0 / 105.0, -1.0 / 280.0)

BZ = 8
HALO = 4
INTERPRET = False
HI = lax.Precision.HIGHEST


def band_matrices(n):
    ms = np.zeros((n, n), np.float32)
    mg = np.zeros((n, n), np.float32)
    for i in range(n):
        for k in range(1, 5):
            for j, sign in ((i + k, 1.0), (i - k, -1.0)):
                if 0 <= j < n:
                    ms[i, j] = SECOND[k]
                    mg[i, j] = sign * FIRST[k]
    return ms, mg


def halo_depth_many(fields):
    count = lax.axis_size("slab")
    ends = count - 1
    heads = jnp.concatenate([f[:HALO] for f in fields], axis=1)
    tails = jnp.concatenate([f[f.shape[0] - HALO:] for f in fields], axis=1)
    above = lax.ppermute(tails, "slab", [(i, i + 1) for i in range(ends)])
    below = lax.ppermute(heads, "slab", [(i + 1, i) for i in range(ends)])
    outs = []
    at = 0
    for f in fields:
        w = f.shape[1]
        outs.append(jnp.concatenate([above[:, at:at + w], f, below[:, at:at + w]], axis=0))
        at += w
    return outs


def ring_gather(x, bounds):
    n = lax.axis_size("probe")
    rings = n // 2
    p = lax.axis_index("probe")
    partner = lax.ppermute(x, "probe", [(i, i ^ 1) for i in range(n)])
    pair = jnp.concatenate([x, partner], 1)
    ahead = [(i, (i + 2) % n) for i in range(n)]
    behind = [(i, (i - 2) % n) for i in range(n)]
    by_offset = {0: pair}
    fwd = pair
    bwd = pair
    half = rings // 2
    for k in range(1, half):
        fwd = lax.ppermute(fwd, "probe", ahead)
        bwd = lax.ppermute(bwd, "probe", behind)
        by_offset[-k % rings] = fwd
        by_offset[k] = bwd
    cut = x.shape[0] // 2
    far = jnp.concatenate(
        [lax.ppermute(fwd[:cut], "probe", ahead), lax.ppermute(bwd[cut:], "probe", behind)], axis=0
    )
    by_offset[half] = far
    width = pair.shape[1]
    strip = x.shape[1]
    zpos = p // 2
    parity = p % 2
    outs = []
    for lo, hi in bounds:
        buf = jnp.zeros((hi - lo, rings * width, x.shape[2]), x.dtype)
        for d in range(rings):
            at = ((zpos + d) % rings) * width
            chunk = by_offset[d][lo:hi]
            buf = lax.dynamic_update_slice_in_dim(buf, chunk[:, :strip], at + parity * strip, 1)
            buf = lax.dynamic_update_slice_in_dim(buf, chunk[:, strip:], at + (1 - parity) * strip, 1)
        outs.append(buf)
    return outs


def _ext(win, idx):
    size = win[0].shape[0]
    return win[idx // size][idx % size]


def _depth_terms(win, j, off, rows):
    c = j + HALO

    def at(idx):
        return _ext(win, idx)[off:off + rows]

    whole = _ext(win, c)
    centre = whole[off:off + rows]
    second = (3.0 * SECOND[0]) * centre
    grad = None
    for k in range(1, 5):
        up = at(c + k)
        down = at(c - k)
        second = second + SECOND[k] * (up + down)
        term = FIRST[k] * (up - down)
        grad = term if grad is None else grad + term
    return whole, centre, second, grad


def _slope_kernel(off, lo_ref, hi_ref, mlane_ref, msub_ref, g0_ref, g1_ref, g2_ref):
    n = mlane_ref.shape[0]
    rows = g0_ref.shape[1]
    for j in range(BZ):
        whole, centre, _, grad = _depth_terms((lo_ref, hi_ref), j, off, rows)
        lane = jnp.dot(centre, mlane_ref[...], precision=HI, preferred_element_type=jnp.float32)
        sub = jnp.dot(msub_ref[...], whole, precision=HI, preferred_element_type=jnp.float32)
        g0_ref[j] = grad
        g1_ref[j] = sub[rows:]
        g2_ref[j] = lane[:, n:]


def _image_of(win, j, coef, mlane_ref, msub_ref, off, rows):
    b_ref, g0_ref, g1_ref, g2_ref = coef
    n = mlane_ref.shape[0]
    whole, centre, second, grad = _depth_terms(win, j, off, rows)
    lane = jnp.dot(centre, mlane_ref[...], precision=HI, preferred_element_type=jnp.float32)
    sub = jnp.dot(msub_ref[...], whole, precision=HI, preferred_element_type=jnp.float32)
    second = second + sub[:rows] + lane[:, :n]
    image = (
        b_ref[j] * second
        + g0_ref[j] * grad
        + g1_ref[j] * sub[rows:]
        + g2_ref[j] * lane[:, n:]
    )
    return centre, image


def _op_kernel(flags, *refs):
    with_prev, with_img, want_image, want_step, off = flags
    refs = list(refs)
    lo_ref, hi_ref, b_ref, g0_ref, g1_ref, g2_ref, mlane_ref, msub_ref = refs[:8]
    rest = refs[8:]
    kappa_ref = prev_ref = dk_ref = img_ref = None
    if want_step:
        kappa_ref = rest.pop(0)
        if with_prev:
            prev_ref = rest.pop(0)
        if with_img:
            dk_ref = rest.pop(0)
            img_ref = rest.pop(0)
    outs = rest
    rows = b_ref.shape[1]
    coef = (b_ref, g0_ref, g1_ref, g2_ref)
    for j in range(BZ):
        centre, image = _image_of((lo_ref, hi_ref), j, coef, mlane_ref, msub_ref, off, rows)
        at = 0
        if want_image:
            outs[at][j] = image
            at += 1
        if want_step:
            step = 2.0 * centre + kappa_ref[j] * image
            if with_prev:
                step = step - prev_ref[j]
            if with_img:
                step = step + dk_ref[j] * img_ref[j]
            outs[at][j] = step


def _first_kernel(lo_ref, hi_ref, b_ref, g0_ref, g1_ref, g2_ref, mlane_ref, msub_ref,
                  kappa_ref, prev_ref, part_ref, dk_ref, bg_ref, born_ref):
    rows = b_ref.shape[1]
    coef = (b_ref, g0_ref, g1_ref, g2_ref)
    for j in range(BZ):
        centre, image = _image_of((lo_ref, hi_ref), j, coef, mlane_ref, msub_ref, 0, rows)
        bg_ref[j] = 2.0 * centre - prev_ref[j] + kappa_ref[j] * image
        born_ref[j] = part_ref[j] + dk_ref[j] * image


def _second_kernel(nwin, *refs):
    win1 = refs[:nwin]
    win2 = refs[nwin:2 * nwin]
    b_ref, g0_ref, g1_ref, g2_ref, mlane_ref, msub_ref, kappa_ref, prev_ref, dk_ref = refs[2 * nwin:2 * nwin + 9]
    img_ref, born_ref = refs[-2:]
    rows = b_ref.shape[1]
    coef = (b_ref, g0_ref, g1_ref, g2_ref)
    for j in range(b_ref.shape[0]):
        _, image = _image_of(win1, j, coef, mlane_ref, msub_ref, 0, rows)
        img_ref[j] = image
        centre, own = _image_of(win2, j, coef, mlane_ref, msub_ref, 0, rows)
        born_ref[j] = 2.0 * centre - prev_ref[j] + kappa_ref[j] * own + dk_ref[j] * image


def _specs(rows, n, count):
    blk = pl.BlockSpec((BZ, rows, n), lambda i: (i, 0, 0))
    return [blk] * count


def _ext_specs(rows, n):
    return [
        pl.BlockSpec((BZ, rows, n), lambda i: (i, 0, 0)),
        pl.BlockSpec((BZ, rows, n), lambda i: (i + 1, 0, 0)),
    ]


def _mat_specs(mlane, msub):
    return [
        pl.BlockSpec(mlane.shape, lambda i: (0, 0)),
        pl.BlockSpec(msub.shape, lambda i: (0, 0)),
    ]


PARAMS = pltpu.CompilerParams(vmem_limit_bytes=48 * 1024 * 1024)


def slopes_of(b_ext, mlane, msub):
    depth = b_ext.shape[0] - 2 * HALO
    rows_in = b_ext.shape[1]
    rows = msub.shape[0] // 2
    n = b_ext.shape[2]
    shape = jax.ShapeDtypeStruct((depth, rows, n), jnp.float32)
    return pl.pallas_call(
        functools.partial(_slope_kernel, (rows_in - rows) // 2),
        grid=(depth // BZ,),
        in_specs=_ext_specs(rows_in, n) + _mat_specs(mlane, msub),
        out_specs=_specs(rows, n, 3),
        out_shape=[shape] * 3,
        compiler_params=PARAMS,
        interpret=INTERPRET,
    )(b_ext, b_ext, mlane, msub)


def apply_op(f_ext, b, slopes, mlane, msub, kappa=None, prev=None, dk=None, img=None, want_image=False):
    depth = f_ext.shape[0] - 2 * HALO
    rows_in = f_ext.shape[1]
    rows = b.shape[1]
    n = f_ext.shape[2]
    off = (rows_in - rows) // 2
    want_step = kappa is not None
    with_prev = prev is not None
    with_img = img is not None
    args = [f_ext, f_ext, b, *slopes, mlane, msub]
    in_specs = _ext_specs(rows_in, n) + _specs(rows, n, 4) + _mat_specs(mlane, msub)
    if want_step:
        extra = [kappa] + ([prev] if with_prev else []) + ([dk, img] if with_img else [])
        args += extra
        in_specs += _specs(rows, n, len(extra))
    n_out = int(want_image) + int(want_step)
    shape = jax.ShapeDtypeStruct((depth, rows, n), jnp.float32)
    outs = pl.pallas_call(
        functools.partial(_op_kernel, (with_prev, with_img, want_image, want_step, off)),
        grid=(depth // BZ,),
        in_specs=in_specs,
        out_specs=_specs(rows, n, n_out),
        out_shape=[shape] * n_out,
        compiler_params=PARAMS,
        interpret=INTERPRET,
    )(*args)
    return outs


def first_step(u_cur_ext, b, slopes, mlane, msub, kappa, u_prev, partial, dk):
    depth = u_cur_ext.shape[0] - 2 * HALO
    n = u_cur_ext.shape[2]
    shape = jax.ShapeDtypeStruct((depth, n, n), jnp.float32)
    return pl.pallas_call(
        _first_kernel,
        grid=(depth // BZ,),
        in_specs=_ext_specs(n, n) + _specs(n, n, 4) + _mat_specs(mlane, msub) + _specs(n, n, 4),
        out_specs=_specs(n, n, 2),
        out_shape=[shape] * 2,
        compiler_params=PARAMS,
        interpret=INTERPRET,
    )(u_cur_ext, u_cur_ext, b, *slopes, mlane, msub, kappa, u_prev, partial, dk)


QB = HALO


def second_inner(bg, born, b, slopes, mlane, msub, kappa, prev, dk):
    depth = bg.shape[0]
    n = bg.shape[2]
    blocks = depth // QB
    win = [pl.BlockSpec((QB, n, n), lambda i, t=t: (i + t, 0, 0)) for t in range(3)]
    inner = [pl.BlockSpec((QB, n, n), lambda i: (i + 1, 0, 0))]
    shape = jax.ShapeDtypeStruct((depth, n, n), jnp.float32)
    return pl.pallas_call(
        functools.partial(_second_kernel, 3),
        grid=(blocks - 2,),
        in_specs=win * 2 + inner * 4 + _mat_specs(mlane, msub) + inner * 3,
        out_specs=inner * 2,
        out_shape=[shape] * 2,
        compiler_params=PARAMS,
        interpret=INTERPRET,
    )(*([bg] * 3), *([born] * 3), b, *slopes, mlane, msub, kappa, prev, dk)


def _edge_kernel(*refs):
    _second_kernel(3, *refs[:-4], *refs[-2:])


def second_edges(bg_rim, born_rim, b, slopes, mlane, msub, kappa, prev, dk, img, born_out):
    depth = b.shape[0]
    n = b.shape[2]
    last = depth // QB - 1
    win = [pl.BlockSpec((QB, n, n), lambda i, t=t: (3 * i + t, 0, 0)) for t in range(3)]
    edge = [pl.BlockSpec((QB, n, n), lambda i: (i * last, 0, 0))]
    anyspec = [pl.BlockSpec(memory_space=pl.ANY)]
    shape = jax.ShapeDtypeStruct((depth, n, n), jnp.float32)
    return pl.pallas_call(
        _edge_kernel,
        grid=(2,),
        in_specs=win * 2 + edge * 4 + _mat_specs(mlane, msub) + edge * 3 + anyspec * 2,
        out_specs=edge * 2,
        out_shape=[shape] * 2,
        input_output_aliases={15: 0, 16: 1},
        compiler_params=PARAMS,
        interpret=INTERPRET,
    )(*([bg_rim] * 3), *([born_rim] * 3), b, *slopes, mlane, msub, kappa, prev, dk, img, born_out)


def depth_rims(fields):
    count = lax.axis_size("slab")
    ends = count - 1
    heads = jnp.concatenate([f[:HALO] for f in fields], axis=1)
    tails = jnp.concatenate([f[f.shape[0] - HALO:] for f in fields], axis=1)
    above = lax.ppermute(tails, "slab", [(i, i + 1) for i in range(ends)])
    below = lax.ppermute(heads, "slab", [(i + 1, i) for i in range(ends)])
    outs = []
    at = 0
    span = QB + HALO
    for f in fields:
        w = f.shape[1]
        d = f.shape[0]
        outs.append(jnp.concatenate(
            [above[:, at:at + w], f[:span], f[d - span:], below[:, at:at + w]], axis=0))
        at += w
    return outs


def local_body(u_prev, u_cur, buoyancy, kappa, dkappa, du_prev, du_cur):
    n = buoyancy.shape[1]
    strip = u_cur.shape[1]
    offset = lax.axis_index("probe") * strip
    ms, mg = band_matrices(n)
    mlane = jnp.asarray(np.concatenate([ms, mg.T], axis=1))
    msub = jnp.asarray(np.concatenate([ms, mg], axis=0))

    depth = u_cur.shape[0]
    cur_rows = depth + 2 * HALO
    probe_kappa = dkappa[0]
    older = du_prev[0]
    newer = du_cur[0]
    (u_cur_strip_ext,) = halo_depth_many([u_cur])
    buoyancy_ext, newer_ext = halo_depth_many([buoyancy, newer])
    u_cur_ext, u_prev_all = ring_gather(
        jnp.concatenate([u_cur_strip_ext, u_prev], axis=0),
        ((0, cur_rows), (cur_rows, cur_rows + depth)),
    )

    slopes = slopes_of(buoyancy_ext, mlane, msub)

    (partial_first,) = apply_op(newer_ext, buoyancy, slopes, mlane, msub, kappa=kappa, prev=older)

    background_first, born_first = first_step(
        u_cur_ext, buoyancy, slopes, mlane, msub, kappa, u_prev_all, partial_first, probe_kappa
    )

    bg_rim, born_rim = depth_rims([background_first, born_first])
    image_second, born_second = second_inner(
        background_first, born_first, buoyancy, slopes, mlane, msub, kappa, newer, probe_kappa
    )
    image_second, born_second = second_edges(
        bg_rim, born_rim, buoyancy, slopes, mlane, msub, kappa, newer, probe_kappa,
        image_second, born_second,
    )

    def cut_strip(field):
        return lax.dynamic_slice_in_dim(field, offset, strip, 1)

    background_first_strip = cut_strip(background_first)
    background_second = (
        2.0 * background_first_strip - u_cur + cut_strip(kappa) * cut_strip(image_second)
    )
    return background_first_strip, background_second, born_first[None], born_second[None]


def solution(mesh):
    return shard_mapped(mesh)


def shard_mapped(mesh):
    return jax.shard_map(
        local_body,
        mesh=mesh,
        in_specs=(
            P("slab", "probe", None),
            P("slab", "probe", None),
            P("slab", None, None),
            P("slab", None, None),
            P("probe", "slab", None, None),
            P("probe", "slab", None, None),
            P("probe", "slab", None, None),
        ),
        out_specs=(
            P("slab", "probe", None),
            P("slab", "probe", None),
            P("probe", "slab", None, None),
            P("probe", "slab", None, None),
        ),
        check_vma=False,
    )
```
